256 devices in a mesh: tile: 16 (over y, z_hi), spec: 16 (over x, z_lo, core).
Axes of the slice: x: 4, y: 4, z: 8 (z_hi: 4, z_lo: 2; z = z_hi * 2 + z_lo), core: 2. Of those that a mesh axis runs over, the one named last changes fastest.
Arguments:
- latent: bfloat16 [32, 4096, 1024], P(None, ('tile', 'spec')), may hold values from -6 to 6
- basis: bfloat16 [224, 32], replicated, may hold values from -1 to 1
- response: bfloat16 [8, 224], replicated, may hold values from -0.375 to 0.375
- hyper_obs: bfloat16 [224, 1024, 256], P('spec', 'tile'), may hold values from -6 to 6
- multi_obs: bfloat16 [8, 4096, 1024], P(None, ('tile', 'spec')), may hold values from -6 to 6
Outputs:
- z_next: bfloat16 [32, 4096, 1024], P(None, ('tile', 'spec'))
- hs_residual: bfloat16 [224, 1024, 256], P('spec', 'tile')
The draws below stay inside these ranges and needn't reach their ends.
All inputs are finite; a program needn't handle non-finite values.
Results may differ from the reference program's by a relative error of at most 0.0054.
Values may be sent and summed in bfloat16 or wider, within the bound.
No kernel may reach another device: no remote copies, remote signals or barrier semaphores. Data moves between devices by JAX's collectives and lax.ppermute only.
A program may use at most 128 MiB of HBM per device.

```python
import jax
import jax.numpy as jnp
from jax import lax

BANDS = 224
SUBSPACE = 32
MS_BANDS = 8
DECIM = 4
HALO = 128
ROWS_DEV = 256
COLS = 1024
ROWS = 4096
LOW_ROWS = 1024
LOW_COLS = 256
N_TILE = 16
N_SPEC = 16


def steps_of(own_key, dims, cuts, smallest, largest):
    factor_of = 1.0
    for position, parts in cuts:
        heights = jax.random.uniform(jax.random.fold_in(jax.random.fold_in(own_key, 6), position), (parts,), jnp.float32, smallest / len(cuts), largest / len(cuts))
        factor_of = factor_of * jnp.repeat(jnp.exp(heights), dims[position] // parts).reshape((-1,) + (1,) * (len(dims) - 1 - position))
    return factor_of


def bell_draw(stream_key, extent, scale, reach, shards=(), held_as=jnp.bfloat16):
    gain = steps_of(stream_key, extent, shards, -0.22, 0.18) if shards else 1.0
    result = jax.random.normal(stream_key, extent, jnp.float32) * scale * gain
    return jnp.minimum(jnp.maximum(result, -reach), reach).astype(held_as)


def setup_inputs(seed: int = 0) -> dict:
    keys = jax.random.split(jax.random.key(seed), 6)
    latent = bell_draw(keys[0], (SUBSPACE, ROWS, COLS), 1.0, 6.0, ((1, 256),))
    basis = bell_draw(keys[1], (BANDS, SUBSPACE), SUBSPACE ** -0.5, 1.0)
    response = bell_draw(keys[2], (MS_BANDS, BANDS), BANDS ** -0.5, 0.375)
    hyper_obs = bell_draw(keys[3], (BANDS, LOW_ROWS, LOW_COLS), 1.0, 6.0, ((0, 16), (1, 16)))
    multi_obs = bell_draw(keys[4], (MS_BANDS, ROWS, COLS), 1.0, 6.0, ((1, 256),))
    return dict(latent=latent, basis=basis, response=response, hyper_obs=hyper_obs, multi_obs=multi_obs)


step_size = 0.3

def profile(where_at):
    narrow = DECIM / 2.0
    decay_len = 3.0 * HALO / 8.0
    ripple = jnp.cos(where_at * (jnp.pi / 7.0))
    return jnp.exp(-where_at * where_at / (2.0 * narrow * narrow)) + 0.5 * jnp.exp(-jnp.abs(where_at) / decay_len) * ripple * ripple

def kernel_values(offsets):
    every_offset = jnp.arange(-HALO, HALO + 1).astype(jnp.float32)
    energy = jnp.sqrt(jnp.sum(profile(every_offset) ** 2))
    inside = jnp.abs(offsets) <= HALO
    return jnp.where(inside, profile(offsets.astype(jnp.float32)) / energy, 0.0).astype(jnp.bfloat16)

def column_matrix(fine_count, coarse_count):
    fine_cols = jnp.arange(fine_count).astype(jnp.int32)[:, None]
    coarse = jnp.arange(coarse_count).astype(jnp.int32)[None, :]
    return kernel_values(fine_cols - DECIM * coarse)

def row_matrix(rows_local):
    coarse = jnp.arange(rows_local // DECIM).astype(jnp.int32)[:, None]
    padded = jnp.arange(rows_local + 2 * HALO).astype(jnp.int32)[None, :]
    return kernel_values(padded - HALO - DECIM * coarse)

def back_matrix(rows_local):
    fine_rows = jnp.arange(rows_local).astype(jnp.int32)[:, None]
    coarse = jnp.arange(rows_local // DECIM + 2 * (HALO // DECIM)).astype(jnp.int32)[None, :]
    return kernel_values(fine_rows - DECIM * coarse + HALO)

def reference(latent, basis, response, hyper_obs, multi_obs):
    highest = lax.Precision.HIGHEST
    column_kernel = column_matrix(COLS, COLS // DECIM).astype(jnp.float32)
    row_kernel = row_matrix(ROWS_DEV).astype(jnp.float32)
    back_kernel = back_matrix(ROWS_DEV).astype(jnp.float32)
    latent_full = latent.astype(jnp.float32)
    basis_full = basis.astype(jnp.float32)
    response_full = response.astype(jnp.float32)
    group = BANDS // N_SPEC
    coarse_rows = ROWS_DEV // DECIM
    rim_rows = HALO // DECIM
    tiles_all = jnp.arange(N_TILE).astype(jnp.int32)
    groups_all = jnp.arange(N_SPEC).astype(jnp.int32)

    def spectra_of(group_index):
        rows_basis = lax.dynamic_slice_in_dim(basis_full, group_index * group, group, 0)
        field = jnp.einsum('bk,krc->brc', rows_basis, latent_full, precision=highest)
        return lax.optimization_barrier(field.astype(jnp.bfloat16)).astype(jnp.float32)

    def multi_step(running, group_index):
        field = spectra_of(group_index)
        cols_response = lax.dynamic_slice_in_dim(response_full, group_index * group, group, 1)
        return (running + jnp.einsum('mb,brc->mrc', cols_response, field, precision=highest), None)
    running, unused = lax.scan(multi_step, jnp.zeros((MS_BANDS, ROWS, COLS), jnp.float32), groups_all)
    multi_resid = (running - multi_obs.astype(jnp.float32)).astype(jnp.bfloat16)
    multi_wide = lax.optimization_barrier(multi_resid).astype(jnp.float32)

    def blur_down(band_field):
        narrowed = jnp.dot(band_field, column_kernel, precision=highest)
        padded = jnp.pad(narrowed, ((HALO, HALO), (0, 0)))

        def one_tile(tile_index):
            window_rows = lax.dynamic_slice_in_dim(padded, tile_index * ROWS_DEV, ROWS_DEV + 2 * HALO, 0)
            return jnp.dot(row_kernel, window_rows, precision=highest)
        return lax.map(one_tile, tiles_all).reshape(LOW_ROWS, LOW_COLS)

    def spread_up(coarse_field):
        padded = jnp.pad(coarse_field, ((rim_rows, rim_rows), (0, 0)))

        def one_tile(tile_index):
            window_rows = lax.dynamic_slice_in_dim(padded, tile_index * coarse_rows, coarse_rows + 2 * rim_rows, 0)
            return jnp.dot(back_kernel, window_rows, precision=highest)
        rows_back = lax.map(one_tile, tiles_all).reshape(ROWS, LOW_COLS)
        return jnp.dot(rows_back, column_kernel.T, precision=highest)

    def main_step(gradient, group_index):
        field = spectra_of(group_index)
        observed = lax.dynamic_slice_in_dim(hyper_obs, group_index * group, group, 0).astype(jnp.float32)
        hyper_resid = (jax.vmap(blur_down)(field) - observed).astype(jnp.bfloat16)
        resid_wide = lax.optimization_barrier(hyper_resid).astype(jnp.float32)
        spread = jax.vmap(spread_up)(resid_wide)
        spread = lax.optimization_barrier(spread.astype(jnp.bfloat16)).astype(jnp.float32)
        cols_response = lax.dynamic_slice_in_dim(response_full, group_index * group, group, 1)
        multi_back = jnp.einsum('mb,mrc->brc', cols_response, multi_wide, precision=highest)
        spectral = lax.optimization_barrier((spread + multi_back).astype(jnp.bfloat16)).astype(jnp.float32)
        rows_basis = lax.dynamic_slice_in_dim(basis_full, group_index * group, group, 0)
        gradient = gradient + jnp.einsum('bk,brc->krc', rows_basis, spectral, precision=highest)
        return (gradient, hyper_resid)
    gradient, residuals = lax.scan(main_step, jnp.zeros((SUBSPACE, ROWS, COLS), jnp.float32), groups_all)
    z_next = (latent_full - step_size * gradient).astype(jnp.bfloat16)
    return (z_next, residuals.reshape(BANDS, LOW_ROWS, LOW_COLS))
```

```python
import jax
import jax.numpy as jnp
from jax import lax
from jax.sharding import PartitionSpec as P

DECIM = 4
HALO = 128


step_size = 0.3


def with_halo(cells, sides, width):
    for axis, dim in sides:
        count = lax.axis_size(axis)
        ends = count - 1
        head = lax.slice_in_dim(cells, 0, width, axis=dim)
        tail = lax.slice_in_dim(cells, cells.shape[dim] - width, cells.shape[dim], axis=dim)
        cells = jnp.concatenate(
            [
                lax.ppermute(tail, axis, [(i, (i + 1) % count) for i in range(ends)]),
                cells,
                lax.ppermute(head, axis, [((i + 1) % count, i) for i in range(ends)]),
            ],
            axis=dim,
        )
    return cells


def profile(where_at):
    narrow = DECIM / 2.0
    decay_len = 3.0 * HALO / 8.0
    ripple = jnp.cos(where_at * (jnp.pi / 7.0))
    return (
        jnp.exp(-where_at * where_at / (2.0 * narrow * narrow))
        + 0.5 * jnp.exp(-jnp.abs(where_at) / decay_len) * ripple * ripple
    )


def kernel_values(offsets):
    every_offset = jnp.arange(-HALO, HALO + 1).astype(jnp.float32)
    energy = jnp.sqrt(jnp.sum(profile(every_offset) ** 2))
    inside = jnp.abs(offsets) <= HALO
    return jnp.where(inside, profile(offsets.astype(jnp.float32)) / energy, 0.0).astype(
        jnp.bfloat16
    )


def column_matrix(fine_count, coarse_count):
    fine_cols = jnp.arange(fine_count)[:, None]
    coarse = jnp.arange(coarse_count)[None, :]
    return kernel_values(fine_cols - DECIM * coarse)


def row_matrix(rows_local):
    coarse = jnp.arange(rows_local // DECIM)[:, None]
    padded = jnp.arange(rows_local + 2 * HALO)[None, :]
    return kernel_values(padded - HALO - DECIM * coarse)


def back_matrix(rows_local):
    fine_rows = jnp.arange(rows_local)[:, None]
    coarse = jnp.arange(rows_local // DECIM + 2 * (HALO // DECIM))[None, :]
    return kernel_values(fine_rows - DECIM * coarse + HALO)


def shards(latent, basis, response, hyper_obs, multi_obs):
    highest = lax.Precision.HIGHEST
    f32 = jnp.float32
    group = hyper_obs.shape[0]
    rows_dev = hyper_obs.shape[1] * DECIM
    width_cols = latent.shape[2]
    spec_index = lax.axis_index("spec")
    basis_wide = basis.astype(f32)
    basis_own = lax.dynamic_slice_in_dim(basis_wide, spec_index * group, group, 0)
    column_kernel = column_matrix(width_cols, width_cols // DECIM)
    column_wide = column_kernel.astype(f32)

    cols_done = jnp.einsum("qrc,cj->qrj", latent, column_kernel, preferred_element_type=f32)
    coef_rows = lax.all_to_all(cols_done, "spec", split_axis=0, concat_axis=1, tiled=True)
    padded = with_halo(coef_rows, (("tile", 1),), HALO)
    coef_blurred = jnp.einsum(
        "ir,qrj->qij", row_matrix(rows_dev).astype(f32), padded, precision=highest
    )
    coef_all = lax.all_gather(coef_blurred, "spec", axis=0, tiled=True)
    blurred = jnp.einsum("bq,qij->bij", basis_own, coef_all, precision=highest)
    hs_residual = (blurred - hyper_obs.astype(f32)).astype(jnp.bfloat16)

    coef_part = jnp.einsum(
        "bq,bij->qij", basis_own.astype(jnp.bfloat16), hs_residual, preferred_element_type=f32
    )
    coef_resid = lax.psum_scatter(coef_part, "spec", scatter_dimension=0, tiled=True)
    coarse_padded = with_halo(coef_resid, (("tile", 1),), HALO // DECIM)
    rows_back = jnp.einsum(
        "rq,cqj->crj", back_matrix(rows_dev).astype(f32), coarse_padded, precision=highest
    )
    rows_pixel = lax.all_to_all(rows_back, "spec", split_axis=1, concat_axis=0, tiled=True)
    grad_hs = jnp.einsum("qrj,cj->qrc", rows_pixel, column_wide, precision=highest)

    resp_basis = jnp.dot(response.astype(f32), basis_wide, precision=highest)
    multi_pred = jnp.einsum("mq,qrc->mrc", resp_basis, latent.astype(f32), precision=highest)
    multi_resid = (multi_pred - multi_obs.astype(f32)).astype(jnp.bfloat16)
    grad_ms = jnp.einsum(
        "mq,mrc->qrc", resp_basis, multi_resid.astype(f32), precision=highest
    )
    gradient = grad_hs + grad_ms
    z_next = (latent.astype(f32) - step_size * gradient).astype(jnp.bfloat16)
    return (z_next, hs_residual)


def solution(mesh):
    in_specs = (
        P(None, ("tile", "spec"), None),
        P(),
        P(),
        P("spec", "tile", None),
        P(None, ("tile", "spec"), None),
    )
    out_specs = (P(None, ("tile", "spec"), None), P("spec", "tile", None))
    return jax.shard_map(shards, mesh=mesh, in_specs=in_specs, out_specs=out_specs, check_vma=False)
```

```python
import jax
import jax.numpy as jnp
from jax import lax
from jax.sharding import PartitionSpec as P

DECIM = 4
HALO = 128


step_size = 0.3


def with_halo(cells, sides, width):
    for axis, dim in sides:
        count = lax.axis_size(axis)
        ends = count - 1
        head = lax.slice_in_dim(cells, 0, width, axis=dim)
        tail = lax.slice_in_dim(cells, cells.shape[dim] - width, cells.shape[dim], axis=dim)
        cells = jnp.concatenate(
            [
                lax.ppermute(tail, axis, [(i, (i + 1) % count) for i in range(ends)]),
                cells,
                lax.ppermute(head, axis, [((i + 1) % count, i) for i in range(ends)]),
            ],
            axis=dim,
        )
    return cells


def profile(where_at):
    narrow = DECIM / 2.0
    decay_len = 3.0 * HALO / 8.0
    ripple = jnp.cos(where_at * (jnp.pi / 7.0))
    return (
        jnp.exp(-where_at * where_at / (2.0 * narrow * narrow))
        + 0.5 * jnp.exp(-jnp.abs(where_at) / decay_len) * ripple * ripple
    )


def kernel_values(offsets):
    every_offset = jnp.arange(-HALO, HALO + 1).astype(jnp.float32)
    energy = jnp.sqrt(jnp.sum(profile(every_offset) ** 2))
    inside = jnp.abs(offsets) <= HALO
    return jnp.where(inside, profile(offsets.astype(jnp.float32)) / energy, 0.0).astype(
        jnp.bfloat16
    )


def column_matrix(fine_count, coarse_count):
    fine_cols = jnp.arange(fine_count)[:, None]
    coarse = jnp.arange(coarse_count)[None, :]
    return kernel_values(fine_cols - DECIM * coarse)


def row_matrix(rows_local):
    coarse = jnp.arange(rows_local // DECIM)[:, None]
    padded = jnp.arange(rows_local + 2 * HALO)[None, :]
    return kernel_values(padded - HALO - DECIM * coarse)


def back_matrix(rows_local):
    fine_rows = jnp.arange(rows_local)[:, None]
    coarse = jnp.arange(rows_local // DECIM + 2 * (HALO // DECIM))[None, :]
    return kernel_values(fine_rows - DECIM * coarse + HALO)


def shards(latent, basis, response, hyper_obs, multi_obs):
    highest = lax.Precision.HIGHEST
    f32 = jnp.float32
    n_spec = lax.axis_size("spec")
    group, coarse_rows, coarse_cols = hyper_obs.shape
    rows_dev = coarse_rows * DECIM
    subspace, rows_here, width_cols = latent.shape
    chunk = coarse_cols // n_spec
    basis_wide = basis.astype(f32)
    column_kernel = column_matrix(width_cols, coarse_cols)
    column_wide = column_kernel.astype(f32)

    cols_done = jnp.einsum(
        "qrc,csj->sqjr",
        latent,
        column_kernel.reshape(width_cols, n_spec, chunk),
        preferred_element_type=f32,
    )
    tile_rows = lax.all_to_all(cols_done, "spec", split_axis=0, concat_axis=3, tiled=True)[0]
    padded = with_halo(tile_rows, (("tile", 2),), HALO)
    coef_blurred = jnp.einsum(
        "qjr,ir->qji", padded, row_matrix(rows_dev).astype(f32), precision=highest
    )
    blurred = jnp.einsum("bq,qji->bji", basis_wide, coef_blurred, precision=highest)

    obs_split = hyper_obs.reshape(group, coarse_rows, n_spec, chunk).transpose(2, 0, 3, 1)
    obs_cols = lax.all_to_all(obs_split, "spec", split_axis=0, concat_axis=1, tiled=True)[0]
    resid_cols = (blurred - obs_cols.astype(f32)).astype(jnp.bfloat16)

    resid_split = resid_cols.reshape(n_spec, group, chunk, coarse_rows)
    resid_bands = lax.all_to_all(resid_split, "spec", split_axis=0, concat_axis=2, tiled=True)[0]
    hs_residual = resid_bands.transpose(0, 2, 1)

    coef_resid = jnp.einsum("bq,bji->qji", basis, resid_cols, preferred_element_type=f32)
    coarse_padded = with_halo(coef_resid, (("tile", 2),), HALO // DECIM)
    rows_back = jnp.einsum(
        "qjk,rk->qjr", coarse_padded, back_matrix(rows_dev).astype(f32), precision=highest
    )
    back_split = rows_back.reshape(subspace, chunk, n_spec, rows_here).transpose(2, 0, 3, 1)
    rows_pixel = lax.all_to_all(back_split, "spec", split_axis=0, concat_axis=3, tiled=True)[0]
    grad_hs = jnp.einsum("qrj,cj->qrc", rows_pixel, column_wide, precision=highest)

    resp_basis = jnp.dot(response.astype(f32), basis_wide, precision=highest)
    multi_pred = jnp.einsum("mq,qrc->mrc", resp_basis, latent.astype(f32), precision=highest)
    multi_resid = (multi_pred - multi_obs.astype(f32)).astype(jnp.bfloat16)
    grad_ms = jnp.einsum(
        "mq,mrc->qrc", resp_basis, multi_resid.astype(f32), precision=highest
    )
    gradient = grad_hs + grad_ms
    z_next = (latent.astype(f32) - step_size * gradient).astype(jnp.bfloat16)
    return (z_next, hs_residual)


def solution(mesh):
    in_specs = (
        P(None, ("tile", "spec"), None),
        P(),
        P(),
        P("spec", "tile", None),
        P(None, ("tile", "spec"), None),
    )
    out_specs = (P(None, ("tile", "spec"), None), P("spec", "tile", None))
    return jax.shard_map(shards, mesh=mesh, in_specs=in_specs, out_specs=out_specs, check_vma=False)
```

```python
import jax
import jax.numpy as jnp
from jax import lax
from jax.sharding import PartitionSpec as P

DECIM = 4
HALO = 128


step_size = 0.3


def with_halo(cells, sides, width):
    for axis, dim in sides:
        count = lax.axis_size(axis)
        ends = count - 1
        head = lax.slice_in_dim(cells, 0, width, axis=dim)
        tail = lax.slice_in_dim(cells, cells.shape[dim] - width, cells.shape[dim], axis=dim)
        cells = jnp.concatenate(
            [
                lax.ppermute(tail, axis, [(i, (i + 1) % count) for i in range(ends)]),
                cells,
                lax.ppermute(head, axis, [((i + 1) % count, i) for i in range(ends)]),
            ],
            axis=dim,
        )
    return cells


def profile(where_at):
    narrow = DECIM / 2.0
    decay_len = 3.0 * HALO / 8.0
    ripple = jnp.cos(where_at * (jnp.pi / 7.0))
    return (
        jnp.exp(-where_at * where_at / (2.0 * narrow * narrow))
        + 0.5 * jnp.exp(-jnp.abs(where_at) / decay_len) * ripple * ripple
    )


def kernel_values(offsets):
    every_offset = jnp.arange(-HALO, HALO + 1).astype(jnp.float32)
    energy = jnp.sqrt(jnp.sum(profile(every_offset) ** 2))
    inside = jnp.abs(offsets) <= HALO
    return jnp.where(inside, profile(offsets.astype(jnp.float32)) / energy, 0.0).astype(
        jnp.bfloat16
    )


def column_matrix(fine_count, coarse_count):
    fine_cols = jnp.arange(fine_count)[:, None]
    coarse = jnp.arange(coarse_count)[None, :]
    return kernel_values(fine_cols - DECIM * coarse)


def row_matrix(rows_local):
    coarse = jnp.arange(rows_local // DECIM)[:, None]
    padded = jnp.arange(rows_local + 2 * HALO)[None, :]
    return kernel_values(padded - HALO - DECIM * coarse)


def back_matrix(rows_local):
    fine_rows = jnp.arange(rows_local)[:, None]
    coarse = jnp.arange(rows_local // DECIM + 2 * (HALO // DECIM))[None, :]
    return kernel_values(fine_rows - DECIM * coarse + HALO)


def split_dot(spec, wide, narrow):
    high_wide = lax.reduce_precision(wide, exponent_bits=8, mantissa_bits=7)
    high = high_wide.astype(jnp.bfloat16)
    low = (wide - high_wide).astype(jnp.bfloat16)
    f32 = jnp.float32
    return jnp.einsum(spec, high, narrow, preferred_element_type=f32) + jnp.einsum(
        spec, low, narrow, preferred_element_type=f32
    )


def swap(chunks, axis):
    count = chunks.shape[0]
    rows = 8 if chunks.dtype == jnp.float32 else 16
    flat = chunks.reshape(count, rows, -1)
    flat = lax.all_to_all(flat, axis, split_axis=0, concat_axis=0, tiled=True)
    return flat.reshape(chunks.shape)


def shards(latent, basis, response, hyper_obs, multi_obs):
    f32 = jnp.float32
    n_spec = lax.axis_size("spec")
    n_tile = lax.axis_size("tile")
    tile_index = lax.axis_index("tile")
    group, coarse_rows, coarse_cols = hyper_obs.shape
    rows_dev = coarse_rows * DECIM
    rim = HALO // DECIM
    subspace, rows_here, width_cols = latent.shape
    chunk = coarse_cols // n_spec
    column_kernel, row_kernel, back_kernel = lax.optimization_barrier(
        (
            column_matrix(width_cols, coarse_cols),
            row_matrix(rows_dev + 2 * (rows_dev - HALO)),
            back_matrix(rows_dev),
        )
    )

    cols_done = jnp.einsum(
        "qrc,csj->sqjr",
        latent,
        column_kernel.reshape(width_cols, n_spec, chunk),
        preferred_element_type=f32,
    )
    got = swap(cols_done, "spec")
    tile_rows = got.transpose(1, 2, 0, 3).reshape(subspace, chunk, rows_dev)
    padded = with_halo(tile_rows, (("tile", 2),), rows_dev)
    coef_blurred = split_dot("qjr,ir->qji", padded, row_kernel)
    blurred = split_dot("qji,bq->bji", coef_blurred, basis)

    obs_split = hyper_obs.reshape(group, coarse_rows, n_spec, chunk).transpose(2, 0, 3, 1)
    obs_cols = swap(obs_split, "spec").reshape(group * n_spec, chunk, coarse_rows)
    obs_wide = with_halo(obs_cols, (("tile", 2),), rim)
    coarse_at = jnp.arange(coarse_rows + 2 * rim) + tile_index * coarse_rows - rim
    inside = (coarse_at >= 0) & (coarse_at < n_tile * coarse_rows)
    resid_wide = jnp.where(inside, blurred - obs_wide.astype(f32), 0.0).astype(jnp.bfloat16)

    resid_cols = lax.slice_in_dim(resid_wide, rim, rim + coarse_rows, axis=2)
    got_bands = swap(resid_cols.reshape(n_spec, group, chunk, coarse_rows), "spec")
    hs_residual = got_bands.transpose(1, 3, 0, 2).reshape(group, coarse_rows, coarse_cols)

    coef_resid = jnp.einsum("bq,bji->qji", basis, resid_wide, preferred_element_type=f32)
    rows_back = split_dot("qjk,rk->qjr", coef_resid, back_kernel)
    back_split = rows_back.reshape(subspace, chunk, n_spec, rows_here).transpose(2, 0, 1, 3)
    got_rows = swap(back_split, "spec")
    rows_pixel = got_rows.transpose(1, 3, 0, 2).reshape(subspace, rows_here, coarse_cols)
    grad_hs = split_dot("qrj,cj->qrc", rows_pixel, column_kernel)

    resp_basis = jnp.dot(response, basis, preferred_element_type=f32)
    multi_pred = split_dot("mq,qrc->mrc", resp_basis, latent)
    multi_resid = (multi_pred - multi_obs.astype(f32)).astype(jnp.bfloat16)
    grad_ms = split_dot("mq,mrc->qrc", resp_basis, multi_resid)
    gradient = grad_hs + grad_ms
    z_next = (latent.astype(f32) - step_size * gradient).astype(jnp.bfloat16)
    return (z_next, hs_residual)


def solution(mesh):
    in_specs = (
        P(None, ("tile", "spec"), None),
        P(),
        P(),
        P("spec", "tile", None),
        P(None, ("tile", "spec"), None),
    )
    out_specs = (P(None, ("tile", "spec"), None), P("spec", "tile", None))
    return jax.shard_map(shards, mesh=mesh, in_specs=in_specs, out_specs=out_specs, check_vma=False)
```

```python
import jax
import jax.numpy as jnp
from jax import lax
from jax.sharding import PartitionSpec as P

DECIM = 4
HALO = 128


step_size = 0.3


def with_halo(cells, sides, width):
    for axis, dim in sides:
        count = lax.axis_size(axis)
        ends = count - 1
        head = lax.slice_in_dim(cells, 0, width, axis=dim)
        tail = lax.slice_in_dim(cells, cells.shape[dim] - width, cells.shape[dim], axis=dim)
        cells = jnp.concatenate(
            [
                lax.ppermute(tail, axis, [(i, (i + 1) % count) for i in range(ends)]),
                cells,
                lax.ppermute(head, axis, [((i + 1) % count, i) for i in range(ends)]),
            ],
            axis=dim,
        )
    return cells


def profile(where_at):
    narrow = DECIM / 2.0
    decay_len = 3.0 * HALO / 8.0
    ripple = jnp.cos(where_at * (jnp.pi / 7.0))
    return (
        jnp.exp(-where_at * where_at / (2.0 * narrow * narrow))
        + 0.5 * jnp.exp(-jnp.abs(where_at) / decay_len) * ripple * ripple
    )


def kernel_values(offsets):
    every_offset = jnp.arange(-HALO, HALO + 1).astype(jnp.float32)
    energy = jnp.sqrt(jnp.sum(profile(every_offset) ** 2))
    inside = jnp.abs(offsets) <= HALO
    return jnp.where(inside, profile(offsets.astype(jnp.float32)) / energy, 0.0).astype(
        jnp.bfloat16
    )


def column_matrix(fine_count, coarse_count):
    fine_cols = jnp.arange(fine_count)[:, None]
    coarse = jnp.arange(coarse_count)[None, :]
    return kernel_values(fine_cols - DECIM * coarse)


def row_matrix(rows_local):
    coarse = jnp.arange(rows_local // DECIM)[:, None]
    padded = jnp.arange(rows_local + 2 * HALO)[None, :]
    return kernel_values(padded - HALO - DECIM * coarse)


def back_matrix(rows_local):
    fine_rows = jnp.arange(rows_local)[:, None]
    coarse = jnp.arange(rows_local // DECIM + 2 * (HALO // DECIM))[None, :]
    return kernel_values(fine_rows - DECIM * coarse + HALO)


def split_dot(spec, wide, narrow):
    high_wide = lax.reduce_precision(wide, exponent_bits=8, mantissa_bits=7)
    high = high_wide.astype(jnp.bfloat16)
    low = (wide - high_wide).astype(jnp.bfloat16)
    f32 = jnp.float32
    return jnp.einsum(spec, high, narrow, preferred_element_type=f32) + jnp.einsum(
        spec, low, narrow, preferred_element_type=f32
    )


def windows(cells, block, width):
    count = cells.shape[0]
    halves = cells.reshape(count, -1, block)
    steps = width // block
    blocks = halves.shape[1] - steps + 1
    return jnp.concatenate([halves[:, k : k + blocks] for k in range(steps)], axis=2)


def shards(latent, basis, response, hyper_obs, multi_obs):
    highest = lax.Precision.HIGHEST
    f32 = jnp.float32
    every = ("tile", "spec")
    n_tile = lax.axis_size("tile")
    n_spec = lax.axis_size("spec")
    group, coarse_rows, coarse_cols = hyper_obs.shape
    rows_dev = coarse_rows * DECIM
    rim = HALO // DECIM
    subspace, rows_here, width_cols = latent.shape
    bands = group * n_spec
    column_kernel = column_matrix(width_cols, coarse_cols)

    cols_done = jnp.einsum("qrc,cj->jqr", latent, column_kernel, preferred_element_type=f32)
    got = lax.all_to_all(cols_done, every, split_axis=0, concat_axis=0, tiled=True)
    column = got.transpose(1, 0, 2).reshape(subspace, -1)
    fine_padded = jnp.pad(column, ((0, 0), (HALO, HALO)))
    fine_windows = windows(fine_padded, rows_dev, rows_dev + 2 * HALO)
    coef_blurred = split_dot("qtr,ir->qti", fine_windows, row_matrix(rows_dev))
    blurred = split_dot("qi,bq->bi", coef_blurred.reshape(subspace, -1), basis)

    obs_split = hyper_obs.transpose(2, 0, 1)
    obs_got = lax.all_to_all(obs_split, every, split_axis=0, concat_axis=0, tiled=True)
    obs_col = obs_got.reshape(n_tile, n_spec, group, coarse_rows).transpose(1, 2, 0, 3)
    resid_col = (blurred - obs_col.reshape(bands, -1).astype(f32)).astype(jnp.bfloat16)

    resid_split = resid_col.reshape(n_spec, group, n_tile, coarse_rows).transpose(2, 0, 1, 3)
    resid_split = resid_split.reshape(n_tile * n_spec, group, coarse_rows)
    resid_got = lax.all_to_all(resid_split, every, split_axis=0, concat_axis=0, tiled=True)
    hs_residual = resid_got.transpose(1, 2, 0)

    coef_resid = jnp.einsum("bq,bi->qi", basis, resid_col, preferred_element_type=f32)
    coarse_padded = jnp.pad(coef_resid, ((0, 0), (rim, rim)))
    coarse_windows = windows(coarse_padded, coarse_rows, coarse_rows + 2 * rim)
    rows_back = split_dot("qtk,rk->qtr", coarse_windows, back_matrix(rows_dev))
    back_split = rows_back.reshape(subspace, -1, rows_here).transpose(1, 0, 2)
    back_got = lax.all_to_all(back_split, every, split_axis=0, concat_axis=0, tiled=True)
    rows_pixel = back_got.transpose(1, 2, 0)
    grad_hs = split_dot("qrj,cj->qrc", rows_pixel, column_kernel)

    basis_wide = basis.astype(f32)
    resp_basis = jnp.dot(response.astype(f32), basis_wide, precision=highest)
    multi_pred = jnp.einsum("mq,qrc->mrc", resp_basis, latent.astype(f32), precision=highest)
    multi_resid = (multi_pred - multi_obs.astype(f32)).astype(jnp.bfloat16)
    grad_ms = jnp.einsum(
        "mq,mrc->qrc", resp_basis, multi_resid.astype(f32), precision=highest
    )
    gradient = grad_hs + grad_ms
    z_next = (latent.astype(f32) - step_size * gradient).astype(jnp.bfloat16)
    return (z_next, hs_residual)


def solution(mesh):
    in_specs = (
        P(None, ("tile", "spec"), None),
        P(),
        P(),
        P("spec", "tile", None),
        P(None, ("tile", "spec"), None),
    )
    out_specs = (P(None, ("tile", "spec"), None), P("spec", "tile", None))
    return jax.shard_map(shards, mesh=mesh, in_specs=in_specs, out_specs=out_specs, check_vma=False)
```

```python
import jax
import jax.numpy as jnp
from jax import lax
from jax.sharding import PartitionSpec as P

DECIM = 4
HALO = 128


step_size = 0.3


def with_halo(cells, sides, width):
    for axis, dim in sides:
        count = lax.axis_size(axis)
        ends = count - 1
        head = lax.slice_in_dim(cells, 0, width, axis=dim)
        tail = lax.slice_in_dim(cells, cells.shape[dim] - width, cells.shape[dim], axis=dim)
        cells = jnp.concatenate(
            [
                lax.ppermute(tail, axis, [(i, (i + 1) % count) for i in range(ends)]),
                cells,
                lax.ppermute(head, axis, [((i + 1) % count, i) for i in range(ends)]),
            ],
            axis=dim,
        )
    return cells


def profile(where_at):
    narrow = DECIM / 2.0
    decay_len = 3.0 * HALO / 8.0
    ripple = jnp.cos(where_at * (jnp.pi / 7.0))
    return (
        jnp.exp(-where_at * where_at / (2.0 * narrow * narrow))
        + 0.5 * jnp.exp(-jnp.abs(where_at) / decay_len) * ripple * ripple
    )


def kernel_values(offsets):
    every_offset = jnp.arange(-HALO, HALO + 1).astype(jnp.float32)
    energy = jnp.sqrt(jnp.sum(profile(every_offset) ** 2))
    inside = jnp.abs(offsets) <= HALO
    return jnp.where(inside, profile(offsets.astype(jnp.float32)) / energy, 0.0).astype(
        jnp.bfloat16
    )


def column_matrix(fine_count, coarse_count):
    fine_cols = jnp.arange(fine_count)[:, None]
    coarse = jnp.arange(coarse_count)[None, :]
    return kernel_values(fine_cols - DECIM * coarse)


def row_matrix(rows_local):
    coarse = jnp.arange(rows_local // DECIM)[:, None]
    padded = jnp.arange(rows_local + 2 * HALO)[None, :]
    return kernel_values(padded - HALO - DECIM * coarse)


def back_matrix(rows_local):
    fine_rows = jnp.arange(rows_local)[:, None]
    coarse = jnp.arange(rows_local // DECIM + 2 * (HALO // DECIM))[None, :]
    return kernel_values(fine_rows - DECIM * coarse + HALO)


def split_dot(spec, wide, narrow):
    high_wide = lax.reduce_precision(wide, exponent_bits=8, mantissa_bits=7)
    high = high_wide.astype(jnp.bfloat16)
    low = (wide - high_wide).astype(jnp.bfloat16)
    f32 = jnp.float32
    return jnp.einsum(spec, high, narrow, preferred_element_type=f32) + jnp.einsum(
        spec, low, narrow, preferred_element_type=f32
    )


def neighbours(parts, axis):
    count = lax.axis_size(axis)
    ends = count - 1
    flat = jnp.concatenate([p.reshape(-1) for p in parts])
    from_prev = lax.ppermute(flat, axis, [(i, i + 1) for i in range(ends)])
    from_next = lax.ppermute(flat, axis, [(i + 1, i) for i in range(ends)])
    out = []
    for got in (from_prev, from_next):
        pieces, at = [], 0
        for p in parts:
            pieces.append(got[at : at + p.size].reshape(p.shape))
            at += p.size
        out.append(pieces)
    return out


def shards(latent, basis, response, hyper_obs, multi_obs):
    highest = lax.Precision.HIGHEST
    f32 = jnp.float32
    bf16 = jnp.bfloat16
    n_spec = lax.axis_size("spec")
    n_tile = lax.axis_size("tile")
    tile_index = lax.axis_index("tile")
    group, coarse_rows, coarse_cols = hyper_obs.shape
    rows_dev = coarse_rows * DECIM
    rim = HALO // DECIM
    subspace, rows_here, width_cols = latent.shape
    chunk = coarse_cols // n_spec
    basis_wide = basis.astype(f32)
    column_kernel = column_matrix(width_cols, coarse_cols)

    cols_done = jnp.einsum(
        "qrc,csj->sqjr",
        latent,
        column_kernel.reshape(width_cols, n_spec, chunk),
        preferred_element_type=f32,
    ).astype(bf16)
    tile_rows = lax.all_to_all(cols_done, "spec", split_axis=0, concat_axis=3, tiled=True)[0]

    obs_split = hyper_obs.reshape(group, coarse_rows, n_spec, chunk).transpose(2, 0, 3, 1)
    obs_cols = lax.all_to_all(obs_split, "spec", split_axis=0, concat_axis=1, tiled=True)[0]

    obs_head = lax.slice_in_dim(obs_cols, 0, rim, axis=2)
    obs_tail = lax.slice_in_dim(obs_cols, coarse_rows - rim, coarse_rows, axis=2)
    (prev_rows, prev_tail, _), (next_rows, _, next_head) = neighbours(
        (tile_rows, obs_tail, obs_head), "tile"
    )
    padded = jnp.concatenate([prev_rows, tile_rows, next_rows], axis=2)
    obs_wide = jnp.concatenate([prev_tail, obs_cols, next_head], axis=2)
    row_kernel = row_matrix(rows_dev + 2 * (rows_dev - HALO))
    coef_blurred = jnp.einsum("qjr,ir->qji", padded, row_kernel, preferred_element_type=f32)
    blurred = split_dot("qji,bq->bji", coef_blurred, basis)
    coarse_at = jnp.arange(coarse_rows + 2 * rim) + tile_index * coarse_rows - rim
    inside = (coarse_at >= 0) & (coarse_at < n_tile * coarse_rows)
    resid_wide = jnp.where(inside, blurred - obs_wide.astype(f32), 0.0).astype(bf16)

    resid_cols = lax.slice_in_dim(resid_wide, rim, rim + coarse_rows, axis=2)
    resid_split = resid_cols.reshape(n_spec, group, chunk, coarse_rows)
    resid_bands = lax.all_to_all(resid_split, "spec", split_axis=0, concat_axis=2, tiled=True)[0]
    hs_residual = resid_bands.transpose(0, 2, 1)

    coef_resid = jnp.einsum("bq,bji->qji", basis, resid_wide, preferred_element_type=f32)
    rows_back = split_dot("qjk,rk->qjr", coef_resid, back_matrix(rows_dev))
    back_split = rows_back.reshape(subspace, chunk, n_spec, rows_here).transpose(2, 0, 3, 1)
    rows_pixel = lax.all_to_all(back_split, "spec", split_axis=0, concat_axis=3, tiled=True)[0]
    grad_hs = split_dot("qrj,cj->qrc", rows_pixel, column_kernel)

    resp_basis = jnp.dot(response.astype(f32), basis_wide, precision=highest)
    multi_pred = jnp.einsum("mq,qrc->mrc", resp_basis, latent.astype(f32), precision=highest)
    multi_resid = (multi_pred - multi_obs.astype(f32)).astype(bf16)
    grad_ms = jnp.einsum(
        "mq,mrc->qrc", resp_basis, multi_resid.astype(f32), precision=highest
    )
    gradient = grad_hs + grad_ms
    z_next = (latent.astype(f32) - step_size * gradient).astype(bf16)
    return (z_next, hs_residual)


def solution(mesh):
    in_specs = (
        P(None, ("tile", "spec"), None),
        P(),
        P(),
        P("spec", "tile", None),
        P(None, ("tile", "spec"), None),
    )
    out_specs = (P(None, ("tile", "spec"), None), P("spec", "tile", None))
    return jax.shard_map(shards, mesh=mesh, in_specs=in_specs, out_specs=out_specs, check_vma=False)
```

```python
import jax
import jax.numpy as jnp
from jax import lax
from jax.sharding import PartitionSpec as P

DECIM = 4
HALO = 128


step_size = 0.3


def with_halo(cells, sides, width):
    for axis, dim in sides:
        count = lax.axis_size(axis)
        ends = count - 1
        head = lax.slice_in_dim(cells, 0, width, axis=dim)
        tail = lax.slice_in_dim(cells, cells.shape[dim] - width, cells.shape[dim], axis=dim)
        cells = jnp.concatenate(
            [
                lax.ppermute(tail, axis, [(i, (i + 1) % count) for i in range(ends)]),
                cells,
                lax.ppermute(head, axis, [((i + 1) % count, i) for i in range(ends)]),
            ],
            axis=dim,
        )
    return cells


def profile(where_at):
    narrow = DECIM / 2.0
    decay_len = 3.0 * HALO / 8.0
    ripple = jnp.cos(where_at * (jnp.pi / 7.0))
    return (
        jnp.exp(-where_at * where_at / (2.0 * narrow * narrow))
        + 0.5 * jnp.exp(-jnp.abs(where_at) / decay_len) * ripple * ripple
    )


def kernel_values(offsets):
    every_offset = jnp.arange(-HALO, HALO + 1).astype(jnp.float32)
    energy = jnp.sqrt(jnp.sum(profile(every_offset) ** 2))
    inside = jnp.abs(offsets) <= HALO
    return jnp.where(inside, profile(offsets.astype(jnp.float32)) / energy, 0.0).astype(
        jnp.bfloat16
    )


def banded(count, width, stride, shift):
    period = width + stride * count
    at = jnp.arange(period)
    offsets = jnp.where(at < width, at, at - period) + shift
    period_values = kernel_values(offsets)
    rows = jnp.tile(period_values, count)[: count * (period - stride)]
    return rows.reshape(count, period - stride)[:, :width]


def split_dot(spec, wide, narrow):
    high_wide = lax.reduce_precision(wide, exponent_bits=8, mantissa_bits=7)
    high = high_wide.astype(jnp.bfloat16)
    low = (wide - high_wide).astype(jnp.bfloat16)
    f32 = jnp.float32
    return jnp.einsum(spec, high, narrow, preferred_element_type=f32) + jnp.einsum(
        spec, low, narrow, preferred_element_type=f32
    )


def shards(latent, basis, response, hyper_obs, multi_obs):
    highest = lax.Precision.HIGHEST
    f32 = jnp.float32
    bf16 = jnp.bfloat16
    n_spec = lax.axis_size("spec")
    n_tile = lax.axis_size("tile")
    tile_index = lax.axis_index("tile")
    group, coarse_rows, coarse_cols = hyper_obs.shape
    rows_dev = coarse_rows * DECIM
    rim = HALO // DECIM
    subspace, rows_here, width_cols = latent.shape
    chunk = coarse_cols // n_spec
    wide_rows = coarse_rows + 2 * rim
    basis_wide = basis.astype(f32)
    column_t = banded(coarse_cols, width_cols, DECIM, 0)
    own_rows = banded(wide_rows, rows_dev, DECIM, HALO)

    cols_done = jnp.einsum(
        "qrc,sjc->sqjr",
        latent,
        column_t.reshape(n_spec, chunk, width_cols),
        preferred_element_type=f32,
    ).astype(bf16)
    tile_rows = lax.all_to_all(cols_done, "spec", split_axis=0, concat_axis=3, tiled=True)[0]

    obs_wide_bands = with_halo(hyper_obs, (("tile", 1),), rim)
    obs_split = obs_wide_bands.reshape(group, wide_rows, n_spec, chunk).transpose(2, 0, 3, 1)
    obs_wide = lax.all_to_all(obs_split, "spec", split_axis=0, concat_axis=1, tiled=True)[0]

    own_part = jnp.einsum("qjr,er->qje", tile_rows, own_rows, preferred_element_type=f32)
    half = wide_rows // 2
    ends = n_tile - 1
    from_prev = lax.ppermute(
        lax.slice_in_dim(own_part, half, wide_rows, axis=2),
        "tile",
        [(i, i + 1) for i in range(ends)],
    )
    from_next = lax.ppermute(
        lax.slice_in_dim(own_part, 0, half, axis=2),
        "tile",
        [(i + 1, i) for i in range(ends)],
    )
    coef_blurred = own_part + jnp.concatenate([from_prev, from_next], axis=2)
    blurred = split_dot("qji,bq->bji", coef_blurred, basis)
    coarse_at = jnp.arange(wide_rows) + tile_index * coarse_rows - rim
    inside = (coarse_at >= 0) & (coarse_at < n_tile * coarse_rows)
    resid_wide = jnp.where(inside, blurred - obs_wide.astype(f32), 0.0).astype(bf16)

    resid_cols = lax.slice_in_dim(resid_wide, rim, rim + coarse_rows, axis=2)
    resid_split = resid_cols.reshape(n_spec, group, chunk, coarse_rows)
    resid_bands = lax.all_to_all(resid_split, "spec", split_axis=0, concat_axis=2, tiled=True)[0]
    hs_residual = resid_bands.transpose(0, 2, 1)

    coef_resid = jnp.einsum("bq,bji->qji", basis, resid_wide, preferred_element_type=f32)
    rows_back = split_dot("qjk,kr->qjr", coef_resid, own_rows)
    back_split = rows_back.reshape(subspace, chunk, n_spec, rows_here).transpose(2, 0, 3, 1)
    rows_pixel = lax.all_to_all(back_split, "spec", split_axis=0, concat_axis=3, tiled=True)[0]
    grad_hs = jnp.einsum(
        "qrj,jc->qrc", rows_pixel, column_t.astype(f32), precision=highest
    )

    resp_basis = jnp.dot(response.astype(f32), basis_wide, precision=highest)
    multi_pred = jnp.einsum("mq,qrc->mrc", resp_basis, latent.astype(f32), precision=highest)
    multi_resid = (multi_pred - multi_obs.astype(f32)).astype(bf16)
    grad_ms = jnp.einsum(
        "mq,mrc->qrc", resp_basis, multi_resid.astype(f32), precision=highest
    )
    gradient = grad_hs + grad_ms
    z_next = (latent.astype(f32) - step_size * gradient).astype(bf16)
    return (z_next, hs_residual)


def solution(mesh):
    in_specs = (
        P(None, ("tile", "spec"), None),
        P(),
        P(),
        P("spec", "tile", None),
        P(None, ("tile", "spec"), None),
    )
    out_specs = (P(None, ("tile", "spec"), None), P("spec", "tile", None))
    return jax.shard_map(shards, mesh=mesh, in_specs=in_specs, out_specs=out_specs, check_vma=False)
```

```python
import jax
import jax.numpy as jnp
from jax import lax
from jax.sharding import PartitionSpec as P

DECIM = 4
HALO = 128


step_size = 0.3


def with_halo(cells, sides, width):
    for axis, dim in sides:
        count = lax.axis_size(axis)
        ends = count - 1
        head = lax.slice_in_dim(cells, 0, width, axis=dim)
        tail = lax.slice_in_dim(cells, cells.shape[dim] - width, cells.shape[dim], axis=dim)
        cells = jnp.concatenate(
            [
                lax.ppermute(tail, axis, [(i, (i + 1) % count) for i in range(ends)]),
                cells,
                lax.ppermute(head, axis, [((i + 1) % count, i) for i in range(ends)]),
            ],
            axis=dim,
        )
    return cells


def profile(where_at):
    narrow = DECIM / 2.0
    decay_len = 3.0 * HALO / 8.0
    ripple = jnp.cos(where_at * (jnp.pi / 7.0))
    return (
        jnp.exp(-where_at * where_at / (2.0 * narrow * narrow))
        + 0.5 * jnp.exp(-jnp.abs(where_at) / decay_len) * ripple * ripple
    )


def kernel_values(offsets):
    every_offset = jnp.arange(-HALO, HALO + 1).astype(jnp.float32)
    energy = jnp.sqrt(jnp.sum(profile(every_offset) ** 2))
    inside = jnp.abs(offsets) <= HALO
    return jnp.where(inside, profile(offsets.astype(jnp.float32)) / energy, 0.0).astype(
        jnp.bfloat16
    )


def banded(count, width, stride, shift):
    period = width + stride * count
    at = jnp.arange(period)
    offsets = jnp.where(at < width, at, at - period) + shift
    period_values = kernel_values(offsets)
    rows = jnp.tile(period_values, count)[: count * (period - stride)]
    return rows.reshape(count, period - stride)[:, :width]


def split_dot(spec, wide, narrow):
    high_wide = lax.reduce_precision(wide, exponent_bits=8, mantissa_bits=7)
    high = high_wide.astype(jnp.bfloat16)
    low = (wide - high_wide).astype(jnp.bfloat16)
    f32 = jnp.float32
    return jnp.einsum(spec, high, narrow, preferred_element_type=f32) + jnp.einsum(
        spec, low, narrow, preferred_element_type=f32
    )


def halves(wide):
    high_wide = lax.reduce_precision(wide, exponent_bits=8, mantissa_bits=7)
    return high_wide.astype(jnp.bfloat16), (wide - high_wide).astype(jnp.bfloat16)


def packed_swap(parts, axis):
    count = parts[0].shape[0]
    flat = jnp.concatenate([p.reshape(count, -1) for p in parts], axis=1)
    got = lax.all_to_all(flat, axis, split_axis=0, concat_axis=0, tiled=True)
    out, at = [], 0
    for p in parts:
        size = p.size // count
        out.append(got[:, at : at + size].reshape(p.shape))
        at += size
    return out


def shards(latent, basis, response, hyper_obs, multi_obs):
    highest = lax.Precision.HIGHEST
    f32 = jnp.float32
    bf16 = jnp.bfloat16
    n_spec = lax.axis_size("spec")
    n_tile = lax.axis_size("tile")
    tile_index = lax.axis_index("tile")
    group, coarse_rows, coarse_cols = hyper_obs.shape
    rows_dev = coarse_rows * DECIM
    rim = HALO // DECIM
    subspace, rows_here, width_cols = latent.shape
    chunk = coarse_cols // n_spec
    wide_rows = coarse_rows + 2 * rim
    half = wide_rows // 2
    basis_wide = basis.astype(f32)
    column_t = banded(coarse_cols, width_cols, DECIM, 0)
    own_rows = banded(wide_rows, rows_dev, DECIM, HALO)

    cols_done = jnp.einsum(
        "qrc,sjc->sqjr",
        latent,
        column_t.reshape(n_spec, chunk, width_cols),
        preferred_element_type=f32,
    ).astype(bf16)
    obs_split = hyper_obs.reshape(group, coarse_rows, n_spec, chunk).transpose(2, 0, 3, 1)
    rows_got, obs_got = packed_swap((cols_done, obs_split), "spec")
    tile_rows = rows_got.transpose(1, 2, 0, 3).reshape(subspace, chunk, rows_dev)
    obs_cols = obs_got.reshape(group * n_spec, chunk, coarse_rows)

    own_part = jnp.einsum("qjr,er->qje", tile_rows, own_rows, preferred_element_type=f32)
    ends = n_tile - 1

    def payload(part, obs_rim):
        high, low = halves(part)
        return jnp.concatenate([high.reshape(-1), low.reshape(-1), obs_rim.reshape(-1)])

    def unpack(got):
        size = subspace * chunk * half
        part = got[:size].astype(f32) + got[size : 2 * size].astype(f32)
        return part.reshape(subspace, chunk, half), got[2 * size :].reshape(-1, chunk, rim)

    to_next = payload(
        lax.slice_in_dim(own_part, half, wide_rows, axis=2),
        lax.slice_in_dim(obs_cols, coarse_rows - rim, coarse_rows, axis=2),
    )
    to_prev = payload(
        lax.slice_in_dim(own_part, 0, half, axis=2), lax.slice_in_dim(obs_cols, 0, rim, axis=2)
    )
    part_prev, rim_prev = unpack(lax.ppermute(to_next, "tile", [(i, i + 1) for i in range(ends)]))
    part_next, rim_next = unpack(lax.ppermute(to_prev, "tile", [(i + 1, i) for i in range(ends)]))
    coef_blurred = own_part + jnp.concatenate([part_prev, part_next], axis=2)
    obs_wide = jnp.concatenate([rim_prev, obs_cols, rim_next], axis=2)
    blurred = split_dot("qji,bq->bji", coef_blurred, basis)
    coarse_at = jnp.arange(wide_rows) + tile_index * coarse_rows - rim
    inside = (coarse_at >= 0) & (coarse_at < n_tile * coarse_rows)
    resid_wide = jnp.where(inside, blurred - obs_wide.astype(f32), 0.0).astype(bf16)

    coef_resid = jnp.einsum("bq,bji->qji", basis, resid_wide, preferred_element_type=f32)
    rows_back = split_dot("qjk,kr->qjr", coef_resid, own_rows).astype(bf16)
    back_split = rows_back.reshape(subspace, chunk, n_spec, rows_here).transpose(2, 0, 1, 3)
    resid_cols = lax.slice_in_dim(resid_wide, rim, rim + coarse_rows, axis=2)
    resid_split = resid_cols.reshape(n_spec, group, chunk, coarse_rows)
    back_got, resid_got = packed_swap((back_split, resid_split), "spec")
    rows_pixel = back_got.transpose(1, 3, 0, 2).reshape(subspace, rows_here, coarse_cols)
    hs_residual = resid_got.transpose(1, 3, 0, 2).reshape(group, coarse_rows, coarse_cols)
    grad_hs = jnp.einsum("qrj,jc->qrc", rows_pixel, column_t, preferred_element_type=f32)

    resp_basis = jnp.dot(response.astype(f32), basis_wide, precision=highest)
    multi_pred = jnp.einsum("mq,qrc->mrc", resp_basis, latent.astype(f32), precision=highest)
    multi_resid = (multi_pred - multi_obs.astype(f32)).astype(bf16)
    grad_ms = jnp.einsum(
        "mq,mrc->qrc", resp_basis, multi_resid.astype(f32), precision=highest
    )
    gradient = grad_hs + grad_ms
    z_next = (latent.astype(f32) - step_size * gradient).astype(bf16)
    return (z_next, hs_residual)


def solution(mesh):
    in_specs = (
        P(None, ("tile", "spec"), None),
        P(),
        P(),
        P("spec", "tile", None),
        P(None, ("tile", "spec"), None),
    )
    out_specs = (P(None, ("tile", "spec"), None), P("spec", "tile", None))
    return jax.shard_map(shards, mesh=mesh, in_specs=in_specs, out_specs=out_specs, check_vma=False)
```

```python
import jax
import jax.numpy as jnp
from jax import lax
from jax.sharding import PartitionSpec as P

DECIM = 4
HALO = 128


step_size = 0.3


def with_halo(cells, sides, width):
    for axis, dim in sides:
        count = lax.axis_size(axis)
        ends = count - 1
        head = lax.slice_in_dim(cells, 0, width, axis=dim)
        tail = lax.slice_in_dim(cells, cells.shape[dim] - width, cells.shape[dim], axis=dim)
        cells = jnp.concatenate(
            [
                lax.ppermute(tail, axis, [(i, (i + 1) % count) for i in range(ends)]),
                cells,
                lax.ppermute(head, axis, [((i + 1) % count, i) for i in range(ends)]),
            ],
            axis=dim,
        )
    return cells


def profile(where_at):
    narrow = DECIM / 2.0
    decay_len = 3.0 * HALO / 8.0
    ripple = jnp.cos(where_at * (jnp.pi / 7.0))
    return (
        jnp.exp(-where_at * where_at / (2.0 * narrow * narrow))
        + 0.5 * jnp.exp(-jnp.abs(where_at) / decay_len) * ripple * ripple
    )


def kernel_values(offsets):
    every_offset = jnp.arange(-HALO, HALO + 1).astype(jnp.float32)
    energy = jnp.sqrt(jnp.sum(profile(every_offset) ** 2))
    inside = jnp.abs(offsets) <= HALO
    return jnp.where(inside, profile(offsets.astype(jnp.float32)) / energy, 0.0).astype(
        jnp.bfloat16
    )


def banded(count, width, stride, shift):
    period = width + stride * count
    at = jnp.arange(period)
    offsets = jnp.where(at < width, at, at - period) + shift
    period_values = kernel_values(offsets)
    rows = jnp.tile(period_values, count)[: count * (period - stride)]
    return rows.reshape(count, period - stride)[:, :width]


def split_dot(spec, wide, narrow):
    high_wide = lax.reduce_precision(wide, exponent_bits=8, mantissa_bits=7)
    high = high_wide.astype(jnp.bfloat16)
    low = (wide - high_wide).astype(jnp.bfloat16)
    f32 = jnp.float32
    return jnp.einsum(spec, high, narrow, preferred_element_type=f32) + jnp.einsum(
        spec, low, narrow, preferred_element_type=f32
    )


def shards(latent, basis, response, hyper_obs, multi_obs):
    highest = lax.Precision.HIGHEST
    f32 = jnp.float32
    bf16 = jnp.bfloat16
    n_spec = lax.axis_size("spec")
    n_tile = lax.axis_size("tile")
    tile_index = lax.axis_index("tile")
    group, coarse_rows, coarse_cols = hyper_obs.shape
    rows_dev = coarse_rows * DECIM
    rim = HALO // DECIM
    subspace, rows_here, width_cols = latent.shape
    chunk = coarse_cols // n_spec
    wide_rows = coarse_rows + 2 * rim
    basis_wide = basis.astype(f32)
    column_t = banded(coarse_cols, width_cols, DECIM, 0)
    own_rows = banded(wide_rows, rows_dev, DECIM, HALO)

    cols_done = jnp.einsum(
        "qrc,sjc->sqjr",
        latent,
        column_t.reshape(n_spec, chunk, width_cols),
        preferred_element_type=f32,
    ).astype(bf16)
    tile_rows = lax.all_to_all(cols_done, "spec", split_axis=0, concat_axis=3, tiled=True)[0]

    obs_wide_bands = with_halo(hyper_obs, (("tile", 1),), rim)
    obs_split = obs_wide_bands.reshape(group, wide_rows, n_spec, chunk).transpose(2, 0, 3, 1)
    obs_wide = lax.all_to_all(obs_split, "spec", split_axis=0, concat_axis=1, tiled=True)[0]

    own_part = jnp.einsum("qjr,er->qje", tile_rows, own_rows, preferred_element_type=f32)
    half = wide_rows // 2
    ends = n_tile - 1
    from_prev = lax.ppermute(
        lax.slice_in_dim(own_part, half, wide_rows, axis=2),
        "tile",
        [(i, i + 1) for i in range(ends)],
    )
    from_next = lax.ppermute(
        lax.slice_in_dim(own_part, 0, half, axis=2),
        "tile",
        [(i + 1, i) for i in range(ends)],
    )
    coef_blurred = own_part + jnp.concatenate([from_prev, from_next], axis=2)
    blurred = split_dot("qji,bq->bji", coef_blurred, basis)
    coarse_at = jnp.arange(wide_rows) + tile_index * coarse_rows - rim
    inside = (coarse_at >= 0) & (coarse_at < n_tile * coarse_rows)
    resid_wide = jnp.where(inside, blurred - obs_wide.astype(f32), 0.0).astype(bf16)

    coef_resid = jnp.einsum("bq,bji->qji", basis, resid_wide, preferred_element_type=f32)
    rows_back = split_dot("qjk,kr->qjr", coef_resid, own_rows).astype(bf16)
    back_split = rows_back.reshape(subspace, chunk, n_spec, rows_here).transpose(2, 0, 3, 1)
    rows_pixel = lax.all_to_all(back_split, "spec", split_axis=0, concat_axis=3, tiled=True)[0]
    grad_hs = jnp.einsum("qrj,jc->qrc", rows_pixel, column_t, preferred_element_type=f32)

    resid_cols = lax.slice_in_dim(resid_wide, rim, rim + coarse_rows, axis=2)
    resid_split = resid_cols.reshape(n_spec, group, chunk, coarse_rows)
    resid_split, _ = lax.optimization_barrier((resid_split, rows_pixel))
    resid_bands = lax.all_to_all(resid_split, "spec", split_axis=0, concat_axis=2, tiled=True)[0]
    hs_residual = resid_bands.transpose(0, 2, 1)

    resp_basis = jnp.dot(response.astype(f32), basis_wide, precision=highest)
    multi_pred = jnp.einsum("mq,qrc->mrc", resp_basis, latent.astype(f32), precision=highest)
    multi_resid = (multi_pred - multi_obs.astype(f32)).astype(bf16)
    grad_ms = jnp.einsum(
        "mq,mrc->qrc", resp_basis, multi_resid.astype(f32), precision=highest
    )
    gradient = grad_hs + grad_ms
    z_next = (latent.astype(f32) - step_size * gradient).astype(bf16)
    return (z_next, hs_residual)


def solution(mesh):
    in_specs = (
        P(None, ("tile", "spec"), None),
        P(),
        P(),
        P("spec", "tile", None),
        P(None, ("tile", "spec"), None),
    )
    out_specs = (P(None, ("tile", "spec"), None), P("spec", "tile", None))
    return jax.shard_map(shards, mesh=mesh, in_specs=in_specs, out_specs=out_specs, check_vma=False)
```

```python
import jax
import jax.numpy as jnp
from jax import lax
from jax.sharding import PartitionSpec as P

DECIM = 4
HALO = 128


step_size = 0.3


def with_halo(cells, sides, width):
    for axis, dim in sides:
        count = lax.axis_size(axis)
        ends = count - 1
        head = lax.slice_in_dim(cells, 0, width, axis=dim)
        tail = lax.slice_in_dim(cells, cells.shape[dim] - width, cells.shape[dim], axis=dim)
        cells = jnp.concatenate(
            [
                lax.ppermute(tail, axis, [(i, (i + 1) % count) for i in range(ends)]),
                cells,
                lax.ppermute(head, axis, [((i + 1) % count, i) for i in range(ends)]),
            ],
            axis=dim,
        )
    return cells


def profile(where_at):
    narrow = DECIM / 2.0
    decay_len = 3.0 * HALO / 8.0
    ripple = jnp.cos(where_at * (jnp.pi / 7.0))
    return (
        jnp.exp(-where_at * where_at / (2.0 * narrow * narrow))
        + 0.5 * jnp.exp(-jnp.abs(where_at) / decay_len) * ripple * ripple
    )


def kernel_values(offsets):
    every_offset = jnp.arange(-HALO, HALO + 1).astype(jnp.float32)
    energy = jnp.sqrt(jnp.sum(profile(every_offset) ** 2))
    inside = jnp.abs(offsets) <= HALO
    return jnp.where(inside, profile(offsets.astype(jnp.float32)) / energy, 0.0).astype(
        jnp.bfloat16
    )


def banded(count, width, stride, shift):
    period = width + stride * count
    at = jnp.arange(period)
    offsets = jnp.where(at < width, at, at - period) + shift
    period_values = kernel_values(offsets)
    rows = jnp.tile(period_values, count)[: count * (period - stride)]
    return rows.reshape(count, period - stride)[:, :width]


def split_dot(spec, wide, narrow):
    high_wide = lax.reduce_precision(wide, exponent_bits=8, mantissa_bits=7)
    high = high_wide.astype(jnp.bfloat16)
    low = (wide - high_wide).astype(jnp.bfloat16)
    f32 = jnp.float32
    return jnp.einsum(spec, high, narrow, preferred_element_type=f32) + jnp.einsum(
        spec, low, narrow, preferred_element_type=f32
    )


def halves(wide):
    high_wide = lax.reduce_precision(wide, exponent_bits=8, mantissa_bits=7)
    return high_wide.astype(jnp.bfloat16), (wide - high_wide).astype(jnp.bfloat16)


def shards(latent, basis, response, hyper_obs, multi_obs):
    highest = lax.Precision.HIGHEST
    f32 = jnp.float32
    bf16 = jnp.bfloat16
    n_spec = lax.axis_size("spec")
    n_tile = lax.axis_size("tile")
    tile_index = lax.axis_index("tile")
    group, coarse_rows, coarse_cols = hyper_obs.shape
    rows_dev = coarse_rows * DECIM
    rim = HALO // DECIM
    subspace, rows_here, width_cols = latent.shape
    chunk = coarse_cols // n_spec
    wide_rows = coarse_rows + 2 * rim
    basis_wide = basis.astype(f32)
    column_t = banded(coarse_cols, width_cols, DECIM, 0)
    own_rows = banded(wide_rows, rows_dev, DECIM, HALO)

    cols_done = jnp.einsum(
        "qrc,sjc->sqjr",
        latent,
        column_t.reshape(n_spec, chunk, width_cols),
        preferred_element_type=f32,
    ).astype(bf16)
    tile_rows = lax.all_to_all(cols_done, "spec", split_axis=0, concat_axis=3, tiled=True)[0]

    obs_split = hyper_obs.reshape(group, coarse_rows, n_spec, chunk).transpose(2, 0, 3, 1)
    obs_cols = lax.all_to_all(obs_split, "spec", split_axis=0, concat_axis=1, tiled=True)[0]

    own_part = jnp.einsum("qjr,er->qje", tile_rows, own_rows, preferred_element_type=f32)
    half = wide_rows // 2
    ends = n_tile - 1

    def payload(part, obs_rim):
        high, low = halves(part)
        return jnp.concatenate([high.reshape(-1), low.reshape(-1), obs_rim.reshape(-1)])

    def unpack(got):
        size = subspace * chunk * half
        part = got[:size].astype(f32) + got[size : 2 * size].astype(f32)
        return part.reshape(subspace, chunk, half), got[2 * size :].reshape(-1, chunk, rim)

    to_next = payload(
        lax.slice_in_dim(own_part, half, wide_rows, axis=2),
        lax.slice_in_dim(obs_cols, coarse_rows - rim, coarse_rows, axis=2),
    )
    to_prev = payload(
        lax.slice_in_dim(own_part, 0, half, axis=2), lax.slice_in_dim(obs_cols, 0, rim, axis=2)
    )
    part_prev, rim_prev = unpack(lax.ppermute(to_next, "tile", [(i, i + 1) for i in range(ends)]))
    part_next, rim_next = unpack(lax.ppermute(to_prev, "tile", [(i + 1, i) for i in range(ends)]))
    coef_blurred = own_part + jnp.concatenate([part_prev, part_next], axis=2)
    obs_wide = jnp.concatenate([rim_prev, obs_cols, rim_next], axis=2)
    blurred = split_dot("qji,bq->bji", coef_blurred, basis)
    coarse_at = jnp.arange(wide_rows) + tile_index * coarse_rows - rim
    inside = (coarse_at >= 0) & (coarse_at < n_tile * coarse_rows)
    resid_wide = jnp.where(inside, blurred - obs_wide.astype(f32), 0.0).astype(bf16)

    coef_resid = jnp.einsum("bq,bji->qji", basis, resid_wide, preferred_element_type=f32)
    rows_back = split_dot("qjk,kr->qjr", coef_resid, own_rows).astype(bf16)
    back_split = rows_back.reshape(subspace, chunk, n_spec, rows_here).transpose(2, 0, 3, 1)
    rows_pixel = lax.all_to_all(back_split, "spec", split_axis=0, concat_axis=3, tiled=True)[0]
    grad_hs = jnp.einsum("qrj,jc->qrc", rows_pixel, column_t, preferred_element_type=f32)

    resid_cols = lax.slice_in_dim(resid_wide, rim, rim + coarse_rows, axis=2)
    resid_split = resid_cols.reshape(n_spec, group, chunk, coarse_rows)
    resid_split, _ = lax.optimization_barrier((resid_split, rows_pixel))
    resid_bands = lax.all_to_all(resid_split, "spec", split_axis=0, concat_axis=2, tiled=True)[0]
    hs_residual = resid_bands.transpose(0, 2, 1)

    resp_basis = jnp.dot(response.astype(f32), basis_wide, precision=highest)
    multi_pred = jnp.einsum("mq,qrc->mrc", resp_basis, latent.astype(f32), precision=highest)
    multi_resid = (multi_pred - multi_obs.astype(f32)).astype(bf16)
    grad_ms = jnp.einsum(
        "mq,mrc->qrc", resp_basis, multi_resid.astype(f32), precision=highest
    )
    gradient = grad_hs + grad_ms
    z_next = (latent.astype(f32) - step_size * gradient).astype(bf16)
    return (z_next, hs_residual)


def solution(mesh):
    in_specs = (
        P(None, ("tile", "spec"), None),
        P(),
        P(),
        P("spec", "tile", None),
        P(None, ("tile", "spec"), None),
    )
    out_specs = (P(None, ("tile", "spec"), None), P("spec", "tile", None))
    return jax.shard_map(shards, mesh=mesh, in_specs=in_specs, out_specs=out_specs, check_vma=False)
```

```python
import jax
import jax.numpy as jnp
from jax import lax
from jax.sharding import PartitionSpec as P

DECIM = 4
HALO = 128


step_size = 0.3


def with_halo(cells, sides, width):
    for axis, dim in sides:
        count = lax.axis_size(axis)
        ends = count - 1
        head = lax.slice_in_dim(cells, 0, width, axis=dim)
        tail = lax.slice_in_dim(cells, cells.shape[dim] - width, cells.shape[dim], axis=dim)
        cells = jnp.concatenate(
            [
                lax.ppermute(tail, axis, [(i, (i + 1) % count) for i in range(ends)]),
                cells,
                lax.ppermute(head, axis, [((i + 1) % count, i) for i in range(ends)]),
            ],
            axis=dim,
        )
    return cells


def profile(where_at):
    narrow = DECIM / 2.0
    decay_len = 3.0 * HALO / 8.0
    ripple = jnp.cos(where_at * (jnp.pi / 7.0))
    return (
        jnp.exp(-where_at * where_at / (2.0 * narrow * narrow))
        + 0.5 * jnp.exp(-jnp.abs(where_at) / decay_len) * ripple * ripple
    )


def kernel_values(offsets):
    every_offset = jnp.arange(-HALO, HALO + 1).astype(jnp.float32)
    energy = jnp.sqrt(jnp.sum(profile(every_offset) ** 2))
    inside = jnp.abs(offsets) <= HALO
    return jnp.where(inside, profile(offsets.astype(jnp.float32)) / energy, 0.0).astype(
        jnp.bfloat16
    )


def banded(count, width, stride, shift):
    period = width + stride * count
    at = jnp.arange(period)
    offsets = jnp.where(at < width, at, at - period) + shift
    period_values = kernel_values(offsets)
    rows = jnp.tile(period_values, count)[: count * (period - stride)]
    return rows.reshape(count, period - stride)[:, :width]


def split_dot(spec, wide, narrow):
    high_wide = lax.reduce_precision(wide, exponent_bits=8, mantissa_bits=7)
    high = high_wide.astype(jnp.bfloat16)
    low = (wide - high_wide).astype(jnp.bfloat16)
    f32 = jnp.float32
    return jnp.einsum(spec, high, narrow, preferred_element_type=f32) + jnp.einsum(
        spec, low, narrow, preferred_element_type=f32
    )


def shards(latent, basis, response, hyper_obs, multi_obs):
    highest = lax.Precision.HIGHEST
    f32 = jnp.float32
    bf16 = jnp.bfloat16
    n_spec = lax.axis_size("spec")
    n_tile = lax.axis_size("tile")
    tile_index = lax.axis_index("tile")
    group, coarse_rows, coarse_cols = hyper_obs.shape
    rows_dev = coarse_rows * DECIM
    rim = HALO // DECIM
    subspace, rows_here, width_cols = latent.shape
    chunk = coarse_cols // n_spec
    wide_rows = coarse_rows + 2 * rim
    basis_wide = basis.astype(f32)
    column_t = banded(coarse_cols, width_cols, DECIM, 0)
    own_rows = banded(wide_rows, rows_dev, DECIM, HALO)

    cols_done = jnp.einsum(
        "qrc,sjc->sqjr",
        latent,
        column_t.reshape(n_spec, chunk, width_cols),
        preferred_element_type=f32,
    ).astype(bf16)
    tile_rows = lax.all_to_all(cols_done, "spec", split_axis=0, concat_axis=3, tiled=True)[0]

    own_part = jnp.einsum("qjr,er->qje", tile_rows, own_rows, preferred_element_type=f32)
    ends = n_tile - 1
    to_next = lax.slice_in_dim(own_part, wide_rows - rim, wide_rows, axis=2)
    to_prev = lax.slice_in_dim(own_part, 0, rim, axis=2)

    obs_split = hyper_obs.reshape(group, coarse_rows, n_spec, chunk).transpose(2, 0, 3, 1)
    obs_split, to_next, to_prev = lax.optimization_barrier((obs_split, to_next, to_prev))
    part_prev = lax.ppermute(to_next, "tile", [(i, i + 1) for i in range(ends)])
    part_next = lax.ppermute(to_prev, "tile", [(i + 1, i) for i in range(ends)])
    obs_cols = lax.all_to_all(obs_split, "spec", split_axis=0, concat_axis=1, tiled=True)[0]
    coef_blurred = lax.slice_in_dim(own_part, rim, rim + coarse_rows, axis=2) + jnp.concatenate(
        [part_prev, part_next], axis=2
    )
    blurred = split_dot("qji,bq->bji", coef_blurred, basis)
    resid_cols = (blurred - obs_cols.astype(f32)).astype(bf16)

    resid_split = resid_cols.reshape(n_spec, group, chunk, coarse_rows)
    resid_bands = lax.all_to_all(resid_split, "spec", split_axis=0, concat_axis=2, tiled=True)[0]
    hs_residual = resid_bands.transpose(0, 2, 1)

    coef_resid = jnp.einsum("bq,bji->qji", basis, resid_cols, preferred_element_type=f32)
    rim_prev = lax.ppermute(
        lax.slice_in_dim(coef_resid, coarse_rows - rim, coarse_rows, axis=2),
        "tile",
        [(i, i + 1) for i in range(ends)],
    )
    rim_next = lax.ppermute(
        lax.slice_in_dim(coef_resid, 0, rim, axis=2), "tile", [(i + 1, i) for i in range(ends)]
    )
    coef_wide = jnp.concatenate([rim_prev, coef_resid, rim_next], axis=2)
    rows_back = split_dot("qjk,kr->qjr", coef_wide, own_rows).astype(bf16)
    back_split = rows_back.reshape(subspace, chunk, n_spec, rows_here).transpose(2, 0, 3, 1)
    rows_pixel = lax.all_to_all(back_split, "spec", split_axis=0, concat_axis=3, tiled=True)[0]
    grad_hs = jnp.einsum("qrj,jc->qrc", rows_pixel, column_t, preferred_element_type=f32)

    resp_basis = jnp.dot(response.astype(f32), basis_wide, precision=highest)
    multi_pred = jnp.einsum("mq,qrc->mrc", resp_basis, latent.astype(f32), precision=highest)
    multi_resid = (multi_pred - multi_obs.astype(f32)).astype(bf16)
    grad_ms = jnp.einsum(
        "mq,mrc->qrc", resp_basis, multi_resid.astype(f32), precision=highest
    )
    gradient = grad_hs + grad_ms
    z_next = (latent.astype(f32) - step_size * gradient).astype(bf16)
    return (z_next, hs_residual)


def solution(mesh):
    in_specs = (
        P(None, ("tile", "spec"), None),
        P(),
        P(),
        P("spec", "tile", None),
        P(None, ("tile", "spec"), None),
    )
    out_specs = (P(None, ("tile", "spec"), None), P("spec", "tile", None))
    return jax.shard_map(shards, mesh=mesh, in_specs=in_specs, out_specs=out_specs, check_vma=False)
```

```python
import jax
import jax.numpy as jnp
from jax import lax
from jax.sharding import PartitionSpec as P

DECIM = 4
HALO = 128


step_size = 0.3


def with_halo(cells, sides, width):
    for axis, dim in sides:
        count = lax.axis_size(axis)
        ends = count - 1
        head = lax.slice_in_dim(cells, 0, width, axis=dim)
        tail = lax.slice_in_dim(cells, cells.shape[dim] - width, cells.shape[dim], axis=dim)
        cells = jnp.concatenate(
            [
                lax.ppermute(tail, axis, [(i, (i + 1) % count) for i in range(ends)]),
                cells,
                lax.ppermute(head, axis, [((i + 1) % count, i) for i in range(ends)]),
            ],
            axis=dim,
        )
    return cells


def profile(where_at):
    narrow = DECIM / 2.0
    decay_len = 3.0 * HALO / 8.0
    ripple = jnp.cos(where_at * (jnp.pi / 7.0))
    return (
        jnp.exp(-where_at * where_at / (2.0 * narrow * narrow))
        + 0.5 * jnp.exp(-jnp.abs(where_at) / decay_len) * ripple * ripple
    )


def kernel_values(offsets):
    every_offset = jnp.arange(-HALO, HALO + 1).astype(jnp.float32)
    energy = jnp.sqrt(jnp.sum(profile(every_offset) ** 2))
    inside = jnp.abs(offsets) <= HALO
    return jnp.where(inside, profile(offsets.astype(jnp.float32)) / energy, 0.0).astype(
        jnp.bfloat16
    )


def banded(count, width, stride, shift):
    period = width + stride * count
    at = jnp.arange(period)
    offsets = jnp.where(at < width, at, at - period) + shift
    period_values = kernel_values(offsets)
    rows = jnp.tile(period_values, count)[: count * (period - stride)]
    return rows.reshape(count, period - stride)[:, :width]


def split_dot(spec, wide, narrow):
    high_wide = lax.reduce_precision(wide, exponent_bits=8, mantissa_bits=7)
    high = high_wide.astype(jnp.bfloat16)
    low = (wide - high_wide).astype(jnp.bfloat16)
    f32 = jnp.float32
    return jnp.einsum(spec, high, narrow, preferred_element_type=f32) + jnp.einsum(
        spec, low, narrow, preferred_element_type=f32
    )


def shards(latent, basis, response, hyper_obs, multi_obs):
    highest = lax.Precision.HIGHEST
    f32 = jnp.float32
    bf16 = jnp.bfloat16
    n_spec = lax.axis_size("spec")
    n_tile = lax.axis_size("tile")
    tile_index = lax.axis_index("tile")
    group, coarse_rows, coarse_cols = hyper_obs.shape
    rows_dev = coarse_rows * DECIM
    rim = HALO // DECIM
    subspace, rows_here, width_cols = latent.shape
    chunk = coarse_cols // n_spec
    wide_rows = coarse_rows + 2 * rim
    basis_wide = basis.astype(f32)
    column_t = banded(coarse_cols, width_cols, DECIM, 0)
    own_rows = banded(wide_rows, rows_dev, DECIM, HALO)

    cols_done = jnp.einsum(
        "qrc,sjc->sqjr",
        latent,
        column_t.reshape(n_spec, chunk, width_cols),
        preferred_element_type=f32,
    ).astype(bf16)
    tile_rows = lax.all_to_all(cols_done, "spec", split_axis=0, concat_axis=3, tiled=True)[0]

    resp_basis = jnp.dot(response.astype(f32), basis_wide, precision=highest)
    multi_pred = jnp.einsum("mq,qrc->mrc", resp_basis, latent.astype(f32), precision=highest)
    multi_resid = (multi_pred - multi_obs.astype(f32)).astype(bf16)
    grad_ms = jnp.einsum(
        "mq,mrc->qrc", resp_basis, multi_resid.astype(f32), precision=highest
    )
    z_base = latent.astype(f32) - step_size * grad_ms

    obs_wide_bands = with_halo(hyper_obs, (("tile", 1),), rim)
    obs_split = obs_wide_bands.reshape(group, wide_rows, n_spec, chunk).transpose(2, 0, 3, 1)
    obs_wide = lax.all_to_all(obs_split, "spec", split_axis=0, concat_axis=1, tiled=True)[0]

    own_part = jnp.einsum("qjr,er->qje", tile_rows, own_rows, preferred_element_type=f32)
    half = wide_rows // 2
    ends = n_tile - 1
    from_prev = lax.ppermute(
        lax.slice_in_dim(own_part, half, wide_rows, axis=2),
        "tile",
        [(i, i + 1) for i in range(ends)],
    )
    from_next = lax.ppermute(
        lax.slice_in_dim(own_part, 0, half, axis=2),
        "tile",
        [(i + 1, i) for i in range(ends)],
    )
    from_prev, from_next, z_base = lax.optimization_barrier((from_prev, from_next, z_base))
    coef_blurred = own_part + jnp.concatenate([from_prev, from_next], axis=2)
    blurred = split_dot("qji,bq->bji", coef_blurred, basis)
    coarse_at = jnp.arange(wide_rows) + tile_index * coarse_rows - rim
    inside = (coarse_at >= 0) & (coarse_at < n_tile * coarse_rows)
    resid_wide = jnp.where(inside, blurred - obs_wide.astype(f32), 0.0).astype(bf16)

    coef_resid = jnp.einsum("bq,bji->qji", basis, resid_wide, preferred_element_type=f32)
    rows_back = split_dot("qjk,kr->qjr", coef_resid, own_rows).astype(bf16)
    back_split = rows_back.reshape(subspace, chunk, n_spec, rows_here).transpose(2, 0, 3, 1)
    rows_pixel = lax.all_to_all(back_split, "spec", split_axis=0, concat_axis=3, tiled=True)[0]
    grad_hs = jnp.einsum("qrj,jc->qrc", rows_pixel, column_t, preferred_element_type=f32)

    resid_cols = lax.slice_in_dim(resid_wide, rim, rim + coarse_rows, axis=2)
    resid_split = resid_cols.reshape(n_spec, group, chunk, coarse_rows)
    resid_split, _ = lax.optimization_barrier((resid_split, rows_pixel))
    resid_bands = lax.all_to_all(resid_split, "spec", split_axis=0, concat_axis=2, tiled=True)[0]
    hs_residual = resid_bands.transpose(0, 2, 1)

    z_next = (z_base - step_size * grad_hs).astype(bf16)
    return (z_next, hs_residual)


def solution(mesh):
    in_specs = (
        P(None, ("tile", "spec"), None),
        P(),
        P(),
        P("spec", "tile", None),
        P(None, ("tile", "spec"), None),
    )
    out_specs = (P(None, ("tile", "spec"), None), P("spec", "tile", None))
    return jax.shard_map(shards, mesh=mesh, in_specs=in_specs, out_specs=out_specs, check_vma=False)
```

```python
import jax
import jax.numpy as jnp
from jax import lax
from jax.sharding import PartitionSpec as P

DECIM = 4
HALO = 128


step_size = 0.3


def with_halo(cells, sides, width):
    for axis, dim in sides:
        count = lax.axis_size(axis)
        ends = count - 1
        head = lax.slice_in_dim(cells, 0, width, axis=dim)
        tail = lax.slice_in_dim(cells, cells.shape[dim] - width, cells.shape[dim], axis=dim)
        cells = jnp.concatenate(
            [
                lax.ppermute(tail, axis, [(i, (i + 1) % count) for i in range(ends)]),
                cells,
                lax.ppermute(head, axis, [((i + 1) % count, i) for i in range(ends)]),
            ],
            axis=dim,
        )
    return cells


def profile(where_at):
    narrow = DECIM / 2.0
    decay_len = 3.0 * HALO / 8.0
    ripple = jnp.cos(where_at * (jnp.pi / 7.0))
    return (
        jnp.exp(-where_at * where_at / (2.0 * narrow * narrow))
        + 0.5 * jnp.exp(-jnp.abs(where_at) / decay_len) * ripple * ripple
    )


def kernel_values(offsets):
    every_offset = jnp.arange(-HALO, HALO + 1).astype(jnp.float32)
    energy = jnp.sqrt(jnp.sum(profile(every_offset) ** 2))
    inside = jnp.abs(offsets) <= HALO
    return jnp.where(inside, profile(offsets.astype(jnp.float32)) / energy, 0.0).astype(
        jnp.bfloat16
    )


def banded(count, width, stride, shift):
    period = width + stride * count
    at = jnp.arange(period)
    offsets = jnp.where(at < width, at, at - period) + shift
    period_values = kernel_values(offsets)
    rows = jnp.tile(period_values, count)[: count * (period - stride)]
    return rows.reshape(count, period - stride)[:, :width]


def split_dot(spec, wide, narrow):
    high_wide = lax.reduce_precision(wide, exponent_bits=8, mantissa_bits=7)
    high = high_wide.astype(jnp.bfloat16)
    low = (wide - high_wide).astype(jnp.bfloat16)
    f32 = jnp.float32
    return jnp.einsum(spec, high, narrow, preferred_element_type=f32) + jnp.einsum(
        spec, low, narrow, preferred_element_type=f32
    )


def shards(latent, basis, response, hyper_obs, multi_obs):
    highest = lax.Precision.HIGHEST
    f32 = jnp.float32
    bf16 = jnp.bfloat16
    n_spec = lax.axis_size("spec")
    n_tile = lax.axis_size("tile")
    tile_index = lax.axis_index("tile")
    group, coarse_rows, coarse_cols = hyper_obs.shape
    rows_dev = coarse_rows * DECIM
    rim = HALO // DECIM
    subspace, rows_here, width_cols = latent.shape
    chunk = coarse_cols // n_spec
    wide_rows = coarse_rows + 2 * rim
    basis_wide = basis.astype(f32)
    column_t = banded(coarse_cols, width_cols, DECIM, 0)
    own_rows = banded(wide_rows, rows_dev, DECIM, HALO)

    cols_done = jnp.einsum(
        "qrc,sjc->sqjr",
        latent,
        column_t.reshape(n_spec, chunk, width_cols),
        preferred_element_type=f32,
    ).astype(bf16)
    tile_rows = lax.all_to_all(cols_done, "spec", split_axis=0, concat_axis=3, tiled=True)[0]

    obs_split = hyper_obs.reshape(group, coarse_rows, n_spec, chunk).transpose(2, 0, 3, 1)
    obs_cols = lax.all_to_all(obs_split, "spec", split_axis=0, concat_axis=1, tiled=True)[0]
    obs_proj = jnp.einsum("bq,bji->qji", basis, obs_cols, preferred_element_type=f32)

    own_part = jnp.einsum("qjr,er->qje", tile_rows, own_rows, preferred_element_type=f32)
    half = wide_rows // 2
    ends = n_tile - 1
    to_next = jnp.concatenate(
        [
            lax.slice_in_dim(own_part, half, wide_rows, axis=2),
            lax.slice_in_dim(obs_proj, coarse_rows - rim, coarse_rows, axis=2),
        ],
        axis=2,
    )
    to_prev = jnp.concatenate(
        [lax.slice_in_dim(own_part, 0, half, axis=2), lax.slice_in_dim(obs_proj, 0, rim, axis=2)],
        axis=2,
    )
    got_prev = lax.ppermute(to_next, "tile", [(i, i + 1) for i in range(ends)])
    got_next = lax.ppermute(to_prev, "tile", [(i + 1, i) for i in range(ends)])
    coef_blurred = own_part + jnp.concatenate(
        [lax.slice_in_dim(got_prev, 0, half, axis=2), lax.slice_in_dim(got_next, 0, half, axis=2)],
        axis=2,
    )

    coef_own = lax.slice_in_dim(coef_blurred, rim, rim + coarse_rows, axis=2)
    blurred = split_dot("qji,bq->bji", coef_own, basis)
    resid_cols = (blurred - obs_cols.astype(f32)).astype(bf16)
    coef_resid = jnp.einsum("bq,bji->qji", basis, resid_cols, preferred_element_type=f32)

    gram = jnp.einsum("bq,bp->qp", basis, basis, preferred_element_type=f32)
    coef_rim = jnp.concatenate(
        [
            lax.slice_in_dim(coef_blurred, 0, rim, axis=2),
            lax.slice_in_dim(coef_blurred, wide_rows - rim, wide_rows, axis=2),
        ],
        axis=2,
    )
    proj_rim = jnp.concatenate(
        [lax.slice_in_dim(got_prev, half, half + rim, axis=2),
         lax.slice_in_dim(got_next, half, half + rim, axis=2)],
        axis=2,
    )
    resid_rim = jnp.einsum("qp,pji->qji", gram, coef_rim, precision=highest) - proj_rim
    rim_prev = jnp.where(tile_index > 0, lax.slice_in_dim(resid_rim, 0, rim, axis=2), 0.0)
    rim_next = jnp.where(
        tile_index < ends, lax.slice_in_dim(resid_rim, rim, 2 * rim, axis=2), 0.0
    )
    coef_wide = jnp.concatenate([rim_prev, coef_resid, rim_next], axis=2)
    rows_back = split_dot("qjk,kr->qjr", coef_wide, own_rows).astype(bf16)
    back_split = rows_back.reshape(subspace, chunk, n_spec, rows_here).transpose(2, 0, 3, 1)
    rows_pixel = lax.all_to_all(back_split, "spec", split_axis=0, concat_axis=3, tiled=True)[0]
    grad_hs = jnp.einsum("qrj,jc->qrc", rows_pixel, column_t, preferred_element_type=f32)

    resid_split = resid_cols.reshape(n_spec, group, chunk, coarse_rows)
    resid_split, _ = lax.optimization_barrier((resid_split, rows_pixel))
    resid_bands = lax.all_to_all(resid_split, "spec", split_axis=0, concat_axis=2, tiled=True)[0]
    hs_residual = resid_bands.transpose(0, 2, 1)

    resp_basis = jnp.dot(response.astype(f32), basis_wide, precision=highest)
    multi_pred = jnp.einsum("mq,qrc->mrc", resp_basis, latent.astype(f32), precision=highest)
    multi_resid = (multi_pred - multi_obs.astype(f32)).astype(bf16)
    grad_ms = jnp.einsum(
        "mq,mrc->qrc", resp_basis, multi_resid.astype(f32), precision=highest
    )
    gradient = grad_hs + grad_ms
    z_next = (latent.astype(f32) - step_size * gradient).astype(bf16)
    return (z_next, hs_residual)


def solution(mesh):
    in_specs = (
        P(None, ("tile", "spec"), None),
        P(),
        P(),
        P("spec", "tile", None),
        P(None, ("tile", "spec"), None),
    )
    out_specs = (P(None, ("tile", "spec"), None), P("spec", "tile", None))
    return jax.shard_map(shards, mesh=mesh, in_specs=in_specs, out_specs=out_specs, check_vma=False)
```

```python
import jax
import jax.numpy as jnp
from jax import lax
from jax.sharding import PartitionSpec as P

DECIM = 4
HALO = 128


step_size = 0.3


def with_halo(cells, sides, width):
    for axis, dim in sides:
        count = lax.axis_size(axis)
        ends = count - 1
        head = lax.slice_in_dim(cells, 0, width, axis=dim)
        tail = lax.slice_in_dim(cells, cells.shape[dim] - width, cells.shape[dim], axis=dim)
        cells = jnp.concatenate(
            [
                lax.ppermute(tail, axis, [(i, (i + 1) % count) for i in range(ends)]),
                cells,
                lax.ppermute(head, axis, [((i + 1) % count, i) for i in range(ends)]),
            ],
            axis=dim,
        )
    return cells


def profile(where_at):
    narrow = DECIM / 2.0
    decay_len = 3.0 * HALO / 8.0
    ripple = jnp.cos(where_at * (jnp.pi / 7.0))
    return (
        jnp.exp(-where_at * where_at / (2.0 * narrow * narrow))
        + 0.5 * jnp.exp(-jnp.abs(where_at) / decay_len) * ripple * ripple
    )


def kernel_values(offsets):
    every_offset = jnp.arange(-HALO, HALO + 1).astype(jnp.float32)
    energy = jnp.sqrt(jnp.sum(profile(every_offset) ** 2))
    inside = jnp.abs(offsets) <= HALO
    return jnp.where(inside, profile(offsets.astype(jnp.float32)) / energy, 0.0).astype(
        jnp.bfloat16
    )


def banded(count, width, stride, shift):
    period = width + stride * count
    at = jnp.arange(period)
    offsets = jnp.where(at < width, at, at - period) + shift
    period_values = kernel_values(offsets)
    rows = jnp.tile(period_values, count)[: count * (period - stride)]
    return rows.reshape(count, period - stride)[:, :width]


def split_dot(spec, wide, narrow):
    high_wide = lax.reduce_precision(wide, exponent_bits=8, mantissa_bits=7)
    high = high_wide.astype(jnp.bfloat16)
    low = (wide - high_wide).astype(jnp.bfloat16)
    f32 = jnp.float32
    return jnp.einsum(spec, high, narrow, preferred_element_type=f32) + jnp.einsum(
        spec, low, narrow, preferred_element_type=f32
    )


def shards(latent, basis, response, hyper_obs, multi_obs):
    highest = lax.Precision.HIGHEST
    f32 = jnp.float32
    bf16 = jnp.bfloat16
    n_spec = lax.axis_size("spec")
    n_tile = lax.axis_size("tile")
    tile_index = lax.axis_index("tile")
    group, coarse_rows, coarse_cols = hyper_obs.shape
    rows_dev = coarse_rows * DECIM
    rim = HALO // DECIM
    subspace, rows_here, width_cols = latent.shape
    chunk = coarse_cols // n_spec
    wide_rows = coarse_rows + 2 * rim
    basis_wide = basis.astype(f32)
    column_t = banded(coarse_cols, width_cols, DECIM, 0)
    own_rows = banded(wide_rows, rows_dev, DECIM, HALO)

    obs_split = hyper_obs.reshape(group, coarse_rows, n_spec, chunk).transpose(2, 0, 3, 1)
    obs_cols = lax.all_to_all(obs_split, "spec", split_axis=0, concat_axis=1, tiled=True)[0]
    obs_proj = jnp.einsum("bq,bji->qji", basis, obs_cols, preferred_element_type=f32)

    latent_now, obs_cols = lax.optimization_barrier((latent, obs_cols))

    cols_done = jnp.einsum(
        "qrc,sjc->sqjr",
        latent_now,
        column_t.reshape(n_spec, chunk, width_cols),
        preferred_element_type=f32,
    ).astype(bf16)
    tile_rows = lax.all_to_all(cols_done, "spec", split_axis=0, concat_axis=3, tiled=True)[0]

    own_part = jnp.einsum("qjr,er->qje", tile_rows, own_rows, preferred_element_type=f32)
    half = wide_rows // 2
    ends = n_tile - 1
    to_next = jnp.concatenate(
        [
            lax.slice_in_dim(own_part, half, wide_rows, axis=2),
            lax.slice_in_dim(obs_proj, coarse_rows - rim, coarse_rows, axis=2),
        ],
        axis=2,
    )
    to_prev = jnp.concatenate(
        [lax.slice_in_dim(own_part, 0, half, axis=2), lax.slice_in_dim(obs_proj, 0, rim, axis=2)],
        axis=2,
    )
    got_prev = lax.ppermute(to_next, "tile", [(i, i + 1) for i in range(ends)])
    got_next = lax.ppermute(to_prev, "tile", [(i + 1, i) for i in range(ends)])
    coef_blurred = own_part + jnp.concatenate(
        [lax.slice_in_dim(got_prev, 0, half, axis=2), lax.slice_in_dim(got_next, 0, half, axis=2)],
        axis=2,
    )

    coef_own = lax.slice_in_dim(coef_blurred, rim, rim + coarse_rows, axis=2)
    blurred = split_dot("qji,bq->bji", coef_own, basis)
    resid_cols = (blurred - obs_cols.astype(f32)).astype(bf16)
    coef_resid = jnp.einsum("bq,bji->qji", basis, resid_cols, preferred_element_type=f32)

    gram = jnp.einsum("bq,bp->qp", basis, basis, preferred_element_type=f32)
    coef_rim = jnp.concatenate(
        [
            lax.slice_in_dim(coef_blurred, 0, rim, axis=2),
            lax.slice_in_dim(coef_blurred, wide_rows - rim, wide_rows, axis=2),
        ],
        axis=2,
    )
    proj_rim = jnp.concatenate(
        [lax.slice_in_dim(got_prev, half, half + rim, axis=2),
         lax.slice_in_dim(got_next, half, half + rim, axis=2)],
        axis=2,
    )
    resid_rim = jnp.einsum("qp,pji->qji", gram, coef_rim, precision=highest) - proj_rim
    rim_prev = jnp.where(tile_index > 0, lax.slice_in_dim(resid_rim, 0, rim, axis=2), 0.0)
    rim_next = jnp.where(
        tile_index < ends, lax.slice_in_dim(resid_rim, rim, 2 * rim, axis=2), 0.0
    )
    coef_wide = jnp.concatenate([rim_prev, coef_resid, rim_next], axis=2)
    rows_back = split_dot("qjk,kr->qjr", coef_wide, own_rows).astype(bf16)
    back_split = rows_back.reshape(subspace, chunk, n_spec, rows_here).transpose(2, 0, 3, 1)
    rows_pixel = lax.all_to_all(back_split, "spec", split_axis=0, concat_axis=3, tiled=True)[0]
    grad_hs = jnp.einsum("qrj,jc->qrc", rows_pixel, column_t, preferred_element_type=f32)

    resid_split = resid_cols.reshape(n_spec, group, chunk, coarse_rows)
    resid_split, _ = lax.optimization_barrier((resid_split, rows_pixel))
    resid_bands = lax.all_to_all(resid_split, "spec", split_axis=0, concat_axis=2, tiled=True)[0]
    hs_residual = resid_bands.transpose(0, 2, 1)

    resp_basis = jnp.dot(response.astype(f32), basis_wide, precision=highest)
    multi_pred = jnp.einsum("mq,qrc->mrc", resp_basis, latent.astype(f32), precision=highest)
    multi_resid = (multi_pred - multi_obs.astype(f32)).astype(bf16)
    grad_ms = jnp.einsum(
        "mq,mrc->qrc", resp_basis, multi_resid.astype(f32), precision=highest
    )
    gradient = grad_hs + grad_ms
    z_next = (latent.astype(f32) - step_size * gradient).astype(bf16)
    return (z_next, hs_residual)


def solution(mesh):
    in_specs = (
        P(None, ("tile", "spec"), None),
        P(),
        P(),
        P("spec", "tile", None),
        P(None, ("tile", "spec"), None),
    )
    out_specs = (P(None, ("tile", "spec"), None), P("spec", "tile", None))
    return jax.shard_map(shards, mesh=mesh, in_specs=in_specs, out_specs=out_specs, check_vma=False)
```

```python
import jax
import jax.numpy as jnp
from jax import lax
from jax.sharding import PartitionSpec as P

DECIM = 4
HALO = 128


step_size = 0.3


def with_halo(cells, sides, width):
    for axis, dim in sides:
        count = lax.axis_size(axis)
        ends = count - 1
        head = lax.slice_in_dim(cells, 0, width, axis=dim)
        tail = lax.slice_in_dim(cells, cells.shape[dim] - width, cells.shape[dim], axis=dim)
        cells = jnp.concatenate(
            [
                lax.ppermute(tail, axis, [(i, (i + 1) % count) for i in range(ends)]),
                cells,
                lax.ppermute(head, axis, [((i + 1) % count, i) for i in range(ends)]),
            ],
            axis=dim,
        )
    return cells


def profile(where_at):
    narrow = DECIM / 2.0
    decay_len = 3.0 * HALO / 8.0
    ripple = jnp.cos(where_at * (jnp.pi / 7.0))
    return (
        jnp.exp(-where_at * where_at / (2.0 * narrow * narrow))
        + 0.5 * jnp.exp(-jnp.abs(where_at) / decay_len) * ripple * ripple
    )


def kernel_values(offsets):
    every_offset = jnp.arange(-HALO, HALO + 1).astype(jnp.float32)
    energy = jnp.sqrt(jnp.sum(profile(every_offset) ** 2))
    inside = jnp.abs(offsets) <= HALO
    return jnp.where(inside, profile(offsets.astype(jnp.float32)) / energy, 0.0).astype(
        jnp.bfloat16
    )


def banded(count, width, stride, shift):
    period = width + stride * count
    at = jnp.arange(period)
    offsets = jnp.where(at < width, at, at - period) + shift
    period_values = kernel_values(offsets)
    rows = jnp.tile(period_values, count)[: count * (period - stride)]
    return rows.reshape(count, period - stride)[:, :width]


def split_dot(spec, wide, narrow):
    high_wide = lax.reduce_precision(wide, exponent_bits=8, mantissa_bits=7)
    high = high_wide.astype(jnp.bfloat16)
    low = (wide - high_wide).astype(jnp.bfloat16)
    f32 = jnp.float32
    return jnp.einsum(spec, high, narrow, preferred_element_type=f32) + jnp.einsum(
        spec, low, narrow, preferred_element_type=f32
    )


def shards(latent, basis, response, hyper_obs, multi_obs):
    highest = lax.Precision.HIGHEST
    f32 = jnp.float32
    bf16 = jnp.bfloat16
    n_spec = lax.axis_size("spec")
    n_tile = lax.axis_size("tile")
    tile_index = lax.axis_index("tile")
    group, coarse_rows, coarse_cols = hyper_obs.shape
    rows_dev = coarse_rows * DECIM
    rim = HALO // DECIM
    subspace, rows_here, width_cols = latent.shape
    chunk = coarse_cols // n_spec
    wide_rows = coarse_rows + 2 * rim
    basis_wide = basis.astype(f32)
    column_t = banded(coarse_cols, width_cols, DECIM, 0)
    own_rows = banded(wide_rows, rows_dev, DECIM, HALO)

    cols_done = jnp.einsum(
        "qrc,sjc->sqjr",
        latent,
        column_t.reshape(n_spec, chunk, width_cols),
        preferred_element_type=f32,
    ).astype(bf16)
    tile_rows = lax.all_to_all(cols_done, "spec", split_axis=0, concat_axis=3, tiled=True)[0]

    obs_split = hyper_obs.reshape(group, coarse_rows, n_spec, chunk).transpose(2, 0, 3, 1)
    obs_cols = lax.all_to_all(obs_split, "spec", split_axis=0, concat_axis=1, tiled=True)[0]
    obs_proj = jnp.einsum("bq,bji->qji", basis, obs_cols, preferred_element_type=f32)

    own_part = jnp.einsum("qjr,er->qje", tile_rows, own_rows, preferred_element_type=f32)
    half = wide_rows // 2
    ends = n_tile - 1
    to_next = jnp.concatenate(
        [
            lax.slice_in_dim(own_part, half, wide_rows, axis=2),
            lax.slice_in_dim(obs_proj, coarse_rows - rim, coarse_rows, axis=2),
        ],
        axis=2,
    )
    to_prev = jnp.concatenate(
        [lax.slice_in_dim(own_part, 0, half, axis=2), lax.slice_in_dim(obs_proj, 0, rim, axis=2)],
        axis=2,
    )
    got_prev = lax.ppermute(to_next, "tile", [(i, i + 1) for i in range(ends)])
    got_next = lax.ppermute(to_prev, "tile", [(i + 1, i) for i in range(ends)])
    coef_blurred = own_part + jnp.concatenate(
        [lax.slice_in_dim(got_prev, 0, half, axis=2), lax.slice_in_dim(got_next, 0, half, axis=2)],
        axis=2,
    )

    coef_own = lax.slice_in_dim(coef_blurred, rim, rim + coarse_rows, axis=2)
    blurred = split_dot("qji,bq->bji", coef_own, basis)
    resid_cols = (blurred - obs_cols.astype(f32)).astype(bf16)
    coef_resid = jnp.einsum("bq,bji->qji", basis, resid_cols, preferred_element_type=f32)

    gram = jnp.einsum("bq,bp->qp", basis, basis, preferred_element_type=f32)
    coef_rim = jnp.concatenate(
        [
            lax.slice_in_dim(coef_blurred, 0, rim, axis=2),
            lax.slice_in_dim(coef_blurred, wide_rows - rim, wide_rows, axis=2),
        ],
        axis=2,
    )
    proj_rim = jnp.concatenate(
        [lax.slice_in_dim(got_prev, half, half + rim, axis=2),
         lax.slice_in_dim(got_next, half, half + rim, axis=2)],
        axis=2,
    )
    resid_rim = jnp.einsum("qp,pji->qji", gram, coef_rim, precision=highest) - proj_rim
    rim_prev = jnp.where(tile_index > 0, lax.slice_in_dim(resid_rim, 0, rim, axis=2), 0.0)
    rim_next = jnp.where(
        tile_index < ends, lax.slice_in_dim(resid_rim, rim, 2 * rim, axis=2), 0.0
    )
    coef_wide = jnp.concatenate([rim_prev, coef_resid, rim_next], axis=2)
    back_split = split_dot(
        "qjk,ksr->sqrj", coef_wide, own_rows.reshape(wide_rows, n_spec, rows_here)
    ).astype(bf16)
    rows_pixel = lax.all_to_all(back_split, "spec", split_axis=0, concat_axis=3, tiled=True)[0]
    grad_hs = jnp.einsum("qrj,jc->qrc", rows_pixel, column_t, preferred_element_type=f32)

    resid_split = resid_cols.reshape(n_spec, group, chunk, coarse_rows)
    resid_split, _ = lax.optimization_barrier((resid_split, rows_pixel))
    resid_bands = lax.all_to_all(resid_split, "spec", split_axis=0, concat_axis=2, tiled=True)[0]
    hs_residual = resid_bands.transpose(0, 2, 1)

    resp_basis = jnp.dot(response.astype(f32), basis_wide, precision=highest)
    multi_pred = jnp.einsum("mq,qrc->mrc", resp_basis, latent.astype(f32), precision=highest)
    multi_resid = (multi_pred - multi_obs.astype(f32)).astype(bf16)
    grad_ms = jnp.einsum(
        "mq,mrc->qrc", resp_basis, multi_resid.astype(f32), precision=highest
    )
    gradient = grad_hs + grad_ms
    z_next = (latent.astype(f32) - step_size * gradient).astype(bf16)
    return (z_next, hs_residual)


def solution(mesh):
    in_specs = (
        P(None, ("tile", "spec"), None),
        P(),
        P(),
        P("spec", "tile", None),
        P(None, ("tile", "spec"), None),
    )
    out_specs = (P(None, ("tile", "spec"), None), P("spec", "tile", None))
    return jax.shard_map(shards, mesh=mesh, in_specs=in_specs, out_specs=out_specs, check_vma=False)
```

```python
import jax
import jax.numpy as jnp
from jax import lax
from jax.sharding import PartitionSpec as P

DECIM = 4
HALO = 128


step_size = 0.3


def with_halo(cells, sides, width):
    for axis, dim in sides:
        count = lax.axis_size(axis)
        ends = count - 1
        head = lax.slice_in_dim(cells, 0, width, axis=dim)
        tail = lax.slice_in_dim(cells, cells.shape[dim] - width, cells.shape[dim], axis=dim)
        cells = jnp.concatenate(
            [
                lax.ppermute(tail, axis, [(i, (i + 1) % count) for i in range(ends)]),
                cells,
                lax.ppermute(head, axis, [((i + 1) % count, i) for i in range(ends)]),
            ],
            axis=dim,
        )
    return cells


def profile(where_at):
    narrow = DECIM / 2.0
    decay_len = 3.0 * HALO / 8.0
    ripple = jnp.cos(where_at * (jnp.pi / 7.0))
    return (
        jnp.exp(-where_at * where_at / (2.0 * narrow * narrow))
        + 0.5 * jnp.exp(-jnp.abs(where_at) / decay_len) * ripple * ripple
    )


def kernel_values(offsets):
    every_offset = jnp.arange(-HALO, HALO + 1).astype(jnp.float32)
    energy = jnp.sqrt(jnp.sum(profile(every_offset) ** 2))
    inside = jnp.abs(offsets) <= HALO
    return jnp.where(inside, profile(offsets.astype(jnp.float32)) / energy, 0.0).astype(
        jnp.bfloat16
    )


def banded(count, width, stride, shift):
    period = width + stride * count
    at = jnp.arange(period)
    offsets = jnp.where(at < width, at, at - period) + shift
    period_values = kernel_values(offsets)
    rows = jnp.tile(period_values, count)[: count * (period - stride)]
    return rows.reshape(count, period - stride)[:, :width]


def split_dot(spec, wide, narrow):
    high_wide = lax.reduce_precision(wide, exponent_bits=8, mantissa_bits=7)
    high = high_wide.astype(jnp.bfloat16)
    low = (wide - high_wide).astype(jnp.bfloat16)
    f32 = jnp.float32
    return jnp.einsum(spec, high, narrow, preferred_element_type=f32) + jnp.einsum(
        spec, low, narrow, preferred_element_type=f32
    )


def shards(latent, basis, response, hyper_obs, multi_obs):
    highest = lax.Precision.HIGHEST
    f32 = jnp.float32
    bf16 = jnp.bfloat16
    n_spec = lax.axis_size("spec")
    n_tile = lax.axis_size("tile")
    tile_index = lax.axis_index("tile")
    group, coarse_rows, coarse_cols = hyper_obs.shape
    rows_dev = coarse_rows * DECIM
    rim = HALO // DECIM
    subspace, rows_here, width_cols = latent.shape
    chunk = coarse_cols // n_spec
    wide_rows = coarse_rows + 2 * rim
    basis_wide = basis.astype(f32)
    column_t = banded(coarse_cols, width_cols, DECIM, 0)
    own_rows = banded(wide_rows, rows_dev, DECIM, HALO)

    cols_done = jnp.einsum(
        "qrc,sjc->sqjr",
        latent,
        column_t.reshape(n_spec, chunk, width_cols),
        preferred_element_type=f32,
    ).astype(bf16)
    tile_rows = lax.all_to_all(cols_done, "spec", split_axis=0, concat_axis=3, tiled=True)[0]

    obs_split = hyper_obs.reshape(group, coarse_rows, n_spec, chunk).transpose(2, 0, 3, 1)
    obs_cols = lax.all_to_all(obs_split, "spec", split_axis=0, concat_axis=1, tiled=True)[0]
    resp_basis = jnp.dot(response.astype(f32), basis_wide, precision=highest)
    multi_pred = jnp.einsum("mq,qrc->mrc", resp_basis, latent.astype(f32), precision=highest)
    multi_resid = (multi_pred - multi_obs.astype(f32)).astype(bf16)
    multi_resid, obs_cols = lax.optimization_barrier((multi_resid, obs_cols))
    obs_proj = jnp.einsum("bq,bji->qji", basis, obs_cols, preferred_element_type=f32)

    own_part = jnp.einsum("qjr,er->qje", tile_rows, own_rows, preferred_element_type=f32)
    half = wide_rows // 2
    ends = n_tile - 1
    to_next = jnp.concatenate(
        [
            lax.slice_in_dim(own_part, half, wide_rows, axis=2),
            lax.slice_in_dim(obs_proj, coarse_rows - rim, coarse_rows, axis=2),
        ],
        axis=2,
    )
    to_prev = jnp.concatenate(
        [lax.slice_in_dim(own_part, 0, half, axis=2), lax.slice_in_dim(obs_proj, 0, rim, axis=2)],
        axis=2,
    )
    got_prev = lax.ppermute(to_next, "tile", [(i, i + 1) for i in range(ends)])
    got_next = lax.ppermute(to_prev, "tile", [(i + 1, i) for i in range(ends)])
    coef_blurred = own_part + jnp.concatenate(
        [lax.slice_in_dim(got_prev, 0, half, axis=2), lax.slice_in_dim(got_next, 0, half, axis=2)],
        axis=2,
    )

    coef_own = lax.slice_in_dim(coef_blurred, rim, rim + coarse_rows, axis=2)
    blurred = split_dot("qji,bq->bji", coef_own, basis)
    resid_cols = (blurred - obs_cols.astype(f32)).astype(bf16)
    coef_resid = jnp.einsum("bq,bji->qji", basis, resid_cols, preferred_element_type=f32)

    gram = jnp.einsum("bq,bp->qp", basis, basis, preferred_element_type=f32)
    coef_rim = jnp.concatenate(
        [
            lax.slice_in_dim(coef_blurred, 0, rim, axis=2),
            lax.slice_in_dim(coef_blurred, wide_rows - rim, wide_rows, axis=2),
        ],
        axis=2,
    )
    proj_rim = jnp.concatenate(
        [lax.slice_in_dim(got_prev, half, half + rim, axis=2),
         lax.slice_in_dim(got_next, half, half + rim, axis=2)],
        axis=2,
    )
    resid_rim = jnp.einsum("qp,pji->qji", gram, coef_rim, precision=highest) - proj_rim
    rim_prev = jnp.where(tile_index > 0, lax.slice_in_dim(resid_rim, 0, rim, axis=2), 0.0)
    rim_next = jnp.where(
        tile_index < ends, lax.slice_in_dim(resid_rim, rim, 2 * rim, axis=2), 0.0
    )
    coef_wide = jnp.concatenate([rim_prev, coef_resid, rim_next], axis=2)
    back_split = split_dot(
        "qjk,ksr->sqrj", coef_wide, own_rows.reshape(wide_rows, n_spec, rows_here)
    ).astype(bf16)
    rows_pixel = lax.all_to_all(back_split, "spec", split_axis=0, concat_axis=3, tiled=True)[0]
    grad_hs = jnp.einsum("qrj,jc->qrc", rows_pixel, column_t, preferred_element_type=f32)

    resid_split = resid_cols.reshape(n_spec, group, chunk, coarse_rows)
    resid_split, _ = lax.optimization_barrier((resid_split, rows_pixel))
    resid_bands = lax.all_to_all(resid_split, "spec", split_axis=0, concat_axis=2, tiled=True)[0]
    hs_residual = resid_bands.transpose(0, 2, 1)

    grad_ms = jnp.einsum(
        "mq,mrc->qrc", resp_basis, multi_resid.astype(f32), precision=highest
    )
    gradient = grad_hs + grad_ms
    z_next = (latent.astype(f32) - step_size * gradient).astype(bf16)
    return (z_next, hs_residual)


def solution(mesh):
    in_specs = (
        P(None, ("tile", "spec"), None),
        P(),
        P(),
        P("spec", "tile", None),
        P(None, ("tile", "spec"), None),
    )
    out_specs = (P(None, ("tile", "spec"), None), P("spec", "tile", None))
    return jax.shard_map(shards, mesh=mesh, in_specs=in_specs, out_specs=out_specs, check_vma=False)
```

```python
import jax
import jax.numpy as jnp
from jax import lax
from jax.sharding import PartitionSpec as P

DECIM = 4
HALO = 128


step_size = 0.3


def with_halo(cells, sides, width):
    for axis, dim in sides:
        count = lax.axis_size(axis)
        ends = count - 1
        head = lax.slice_in_dim(cells, 0, width, axis=dim)
        tail = lax.slice_in_dim(cells, cells.shape[dim] - width, cells.shape[dim], axis=dim)
        cells = jnp.concatenate(
            [
                lax.ppermute(tail, axis, [(i, (i + 1) % count) for i in range(ends)]),
                cells,
                lax.ppermute(head, axis, [((i + 1) % count, i) for i in range(ends)]),
            ],
            axis=dim,
        )
    return cells


def profile(where_at):
    narrow = DECIM / 2.0
    decay_len = 3.0 * HALO / 8.0
    ripple = jnp.cos(where_at * (jnp.pi / 7.0))
    return (
        jnp.exp(-where_at * where_at / (2.0 * narrow * narrow))
        + 0.5 * jnp.exp(-jnp.abs(where_at) / decay_len) * ripple * ripple
    )


def kernel_values(offsets):
    every_offset = jnp.arange(-HALO, HALO + 1).astype(jnp.float32)
    energy = jnp.sqrt(jnp.sum(profile(every_offset) ** 2))
    inside = jnp.abs(offsets) <= HALO
    return jnp.where(inside, profile(offsets.astype(jnp.float32)) / energy, 0.0).astype(
        jnp.bfloat16
    )


def banded(count, width, stride, shift):
    period = width + stride * count
    at = jnp.arange(period)
    offsets = jnp.where(at < width, at, at - period) + shift
    period_values = kernel_values(offsets)
    rows = jnp.tile(period_values, count)[: count * (period - stride)]
    return rows.reshape(count, period - stride)[:, :width]


def split_dot(spec, wide, narrow):
    high_wide = lax.reduce_precision(wide, exponent_bits=8, mantissa_bits=7)
    high = high_wide.astype(jnp.bfloat16)
    low = (wide - high_wide).astype(jnp.bfloat16)
    f32 = jnp.float32
    return jnp.einsum(spec, high, narrow, preferred_element_type=f32) + jnp.einsum(
        spec, low, narrow, preferred_element_type=f32
    )


def shards(latent, basis, response, hyper_obs, multi_obs):
    highest = lax.Precision.HIGHEST
    f32 = jnp.float32
    bf16 = jnp.bfloat16
    n_spec = lax.axis_size("spec")
    n_tile = lax.axis_size("tile")
    tile_index = lax.axis_index("tile")
    group, coarse_rows, coarse_cols = hyper_obs.shape
    rows_dev = coarse_rows * DECIM
    rim = HALO // DECIM
    subspace, rows_here, width_cols = latent.shape
    chunk = coarse_cols // n_spec
    wide_rows = coarse_rows + 2 * rim
    basis_wide = basis.astype(f32)
    column_t = banded(coarse_cols, width_cols, DECIM, 0)
    own_rows = banded(wide_rows, rows_dev, DECIM, HALO)

    cols_done = jnp.einsum(
        "qrc,sjc->sqjr",
        latent,
        column_t.reshape(n_spec, chunk, width_cols),
        preferred_element_type=f32,
    ).astype(bf16)
    tile_rows = lax.all_to_all(cols_done, "spec", split_axis=0, concat_axis=3, tiled=True)[0]

    obs_split = hyper_obs.reshape(group, coarse_rows, n_spec, chunk).transpose(2, 0, 3, 1)
    obs_cols = lax.all_to_all(obs_split, "spec", split_axis=0, concat_axis=1, tiled=True)[0]
    resp_basis = jnp.dot(response.astype(f32), basis_wide, precision=highest)
    multi_pred = jnp.einsum("mq,qrc->mrc", resp_basis, latent.astype(f32), precision=highest)
    multi_resid = (multi_pred - multi_obs.astype(f32)).astype(bf16)
    multi_resid, obs_cols = lax.optimization_barrier((multi_resid, obs_cols))
    obs_proj = jnp.einsum("bq,bji->qji", basis, obs_cols, preferred_element_type=f32)

    own_part = jnp.einsum("qjr,er->qje", tile_rows, own_rows, preferred_element_type=f32)
    half = wide_rows // 2
    ends = n_tile - 1
    to_next = jnp.concatenate(
        [
            lax.slice_in_dim(own_part, half, wide_rows, axis=2),
            lax.slice_in_dim(obs_proj, coarse_rows - rim, coarse_rows, axis=2),
        ],
        axis=2,
    )
    to_prev = jnp.concatenate(
        [lax.slice_in_dim(own_part, 0, half, axis=2), lax.slice_in_dim(obs_proj, 0, rim, axis=2)],
        axis=2,
    )
    got_prev = lax.ppermute(to_next, "tile", [(i, i + 1) for i in range(ends)])
    got_next = lax.ppermute(to_prev, "tile", [(i + 1, i) for i in range(ends)])
    grad_ms = jnp.einsum(
        "mq,mrc->qrc", resp_basis, multi_resid.astype(f32), precision=highest
    )
    grad_ms, got_prev, got_next = lax.optimization_barrier((grad_ms, got_prev, got_next))
    coef_blurred = own_part + jnp.concatenate(
        [lax.slice_in_dim(got_prev, 0, half, axis=2), lax.slice_in_dim(got_next, 0, half, axis=2)],
        axis=2,
    )

    coef_own = lax.slice_in_dim(coef_blurred, rim, rim + coarse_rows, axis=2)
    blurred = split_dot("qji,bq->bji", coef_own, basis)
    resid_cols = (blurred - obs_cols.astype(f32)).astype(bf16)
    coef_resid = jnp.einsum("bq,bji->qji", basis, resid_cols, preferred_element_type=f32)

    gram = jnp.einsum("bq,bp->qp", basis, basis, preferred_element_type=f32)
    coef_rim = jnp.concatenate(
        [
            lax.slice_in_dim(coef_blurred, 0, rim, axis=2),
            lax.slice_in_dim(coef_blurred, wide_rows - rim, wide_rows, axis=2),
        ],
        axis=2,
    )
    proj_rim = jnp.concatenate(
        [lax.slice_in_dim(got_prev, half, half + rim, axis=2),
         lax.slice_in_dim(got_next, half, half + rim, axis=2)],
        axis=2,
    )
    resid_rim = jnp.einsum("qp,pji->qji", gram, coef_rim, precision=highest) - proj_rim
    rim_prev = jnp.where(tile_index > 0, lax.slice_in_dim(resid_rim, 0, rim, axis=2), 0.0)
    rim_next = jnp.where(
        tile_index < ends, lax.slice_in_dim(resid_rim, rim, 2 * rim, axis=2), 0.0
    )
    coef_wide = jnp.concatenate([rim_prev, coef_resid, rim_next], axis=2)
    back_split = split_dot(
        "qjk,ksr->sqrj", coef_wide, own_rows.reshape(wide_rows, n_spec, rows_here)
    ).astype(bf16)
    rows_pixel = lax.all_to_all(back_split, "spec", split_axis=0, concat_axis=3, tiled=True)[0]
    grad_hs = jnp.einsum("qrj,jc->qrc", rows_pixel, column_t, preferred_element_type=f32)

    resid_split = resid_cols.reshape(n_spec, group, chunk, coarse_rows)
    resid_split, _ = lax.optimization_barrier((resid_split, rows_pixel))
    resid_bands = lax.all_to_all(resid_split, "spec", split_axis=0, concat_axis=2, tiled=True)[0]
    hs_residual = resid_bands.transpose(0, 2, 1)

    gradient = grad_hs + grad_ms
    z_next = (latent.astype(f32) - step_size * gradient).astype(bf16)
    return (z_next, hs_residual)


def solution(mesh):
    in_specs = (
        P(None, ("tile", "spec"), None),
        P(),
        P(),
        P("spec", "tile", None),
        P(None, ("tile", "spec"), None),
    )
    out_specs = (P(None, ("tile", "spec"), None), P("spec", "tile", None))
    return jax.shard_map(shards, mesh=mesh, in_specs=in_specs, out_specs=out_specs, check_vma=False)
```
